512 devices in a mesh: call: 8 (over z), tm: 64 (over x, y, core).
Axes of the slice: x: 4, y: 8, z: 8, core: 2. Of those that a mesh axis runs over, the one named last changes fastest.
Arguments:
- frames: bfloat16 [8, 8192, 1024], P('call', 'tm'), may hold values from -6 to 6
- lengths: int32 [8], replicated, may hold values from 2048 to 8192, as said below
- ln_attn_gain: float32 [1024], replicated, may hold values from 0.5 to 1.5
- w_qkv: bfloat16 [1024, 3072], P('tm'), may hold values from -0.1875 to 0.1875
- w_out: bfloat16 [1024, 1024], P('tm'), may hold values from -1.5 to 1.5
- ln_conv_gain: float32 [1024], replicated, may hold values from 0.5 to 1.5
- w_pw1: bfloat16 [1024, 2048], P('tm'), may hold values from -0.1875 to 0.1875
- dw_kernel: float32 [9, 1024], replicated, may hold values from -2 to 2
- bn_gain: float32 [1024], replicated, may hold values from 0.5 to 1.5
- bn_bias: float32 [1024], replicated, may hold values from -3 to 3
Outputs:
- attended: bfloat16 [8, 8192, 1024], P('call', 'tm')
- conv_act: bfloat16 [8, 8192, 1024], P('call', 'tm')
The draws below stay inside these ranges and needn't reach their ends.
Inputs may be any that keep to these rules, and one draw needn't show every extreme that they name: `lengths`: valid frames of each call; at least one call of the batch fills all 8192 frames.
All inputs are finite; a program needn't handle non-finite values.
Results may differ from the reference program's by a relative error of at most 0.009.
Values may be sent and summed in bfloat16 or wider, within the bound.
No kernel may reach another device: no remote copies, remote signals or barrier semaphores. Data moves between devices by JAX's collectives and lax.ppermute only.
A program may use at most 64 MiB of HBM per device.

```python
import jax
import jax.numpy as jnp
from jax import lax

D = 1024
HEADS = 16
HEAD_DIM = 64
SPAN = 128
LEFT = 1024
KERNEL = 9
FRAMES = 8192
BATCH = 8


def draw_lengths(key, part):
    drawn = jax.random.randint(jax.random.fold_in(key, 11), (BATCH,), FRAMES // 4, FRAMES + 1, dtype=jnp.int32)
    chosen = jax.random.randint(jax.random.fold_in(key, 12), (), 0, BATCH, dtype=jnp.int32)
    slots = jnp.arange(BATCH, dtype=jnp.int32)
    return jnp.where(slots == chosen, jnp.int32(FRAMES), drawn).astype(jnp.int32)


def levels(stream_key, dims, pieces, least, high):
    level, own = 1.0, jax.random.fold_in(stream_key, 6)
    for axis_at, parts in pieces:
        heights = jnp.exp(jax.random.uniform(jax.random.fold_in(own, axis_at), (parts,), jnp.float32, least / len(pieces), high / len(pieces)))
        level = level * jnp.repeat(heights, dims[axis_at] // parts).reshape([-1 if axis == axis_at else 1 for axis in range(len(dims))])
    return level


def scatter_about(stream_key, shape, scale, limit, split=(), kind=jnp.bfloat16):
    values = scale * jax.random.normal(stream_key, shape, jnp.float32)
    if split:
        values = values * levels(stream_key, shape, split, -0.22, 0.18)
    return jnp.clip(values, -limit, limit).astype(kind)


def setup_inputs(seed: int = 0) -> dict:
    splits = jax.random.split(jax.random.key(seed), 11)
    frames = scatter_about(splits[0], (BATCH, FRAMES, D), 1.0, 6.0, ((0, 8), (1, 64)))
    lengths = draw_lengths(jax.random.fold_in(splits[10], 71), 0)
    ln_attn_gain = jnp.clip(1.0 + 0.1 * jax.random.normal(splits[2], (D,), jnp.float32), 0.5, 1.5)
    w_qkv = scatter_about(splits[3], (D, 3 * D), D ** -0.5, 0.1875, ((0, 64),))
    w_out = scatter_about(splits[4], (D, D), (D // 64) ** -0.5, 1.5, ((0, 64),))
    ln_conv_gain = jnp.clip(1.0 + 0.1 * jax.random.normal(splits[5], (D,), jnp.float32), 0.5, 1.5)
    w_pw1 = scatter_about(splits[6], (D, 2 * D), D ** -0.5, 0.1875, ((0, 64),))
    dw_kernel = scatter_about(splits[7], (KERNEL, D), KERNEL ** -0.5, 2.0, (), jnp.float32)
    bn_gain = jnp.clip(1.0 + 0.1 * jax.random.normal(splits[8], (D,), jnp.float32), 0.5, 1.5)
    bn_bias = scatter_about(splits[9], (D,), 0.5, 3.0, (), jnp.float32)
    return {"frames": frames, "lengths": lengths, "ln_attn_gain": ln_attn_gain, "w_qkv": w_qkv, "w_out": w_out, "ln_conv_gain": ln_conv_gain, "w_pw1": w_pw1, "dw_kernel": dw_kernel, "bn_gain": bn_gain, "bn_bias": bn_bias}


def layer_norm(values, gain_vec):
    wide = values.astype(jnp.float32)
    center = wide - lax.optimization_barrier(jnp.mean(wide, axis=-1, keepdims=True))
    spread = lax.optimization_barrier(jnp.mean(center * center, axis=-1, keepdims=True))
    return center * lax.rsqrt(spread + 1e-05) * gain_vec

def reference(frames, lengths, ln_attn_gain, w_qkv, w_out, ln_conv_gain, w_pw1, dw_kernel, bn_gain, bn_bias):
    positions = jnp.arange(FRAMES, dtype=jnp.int32)
    half = KERNEL // 2

    def first_pass(operands):
        call_frames, length = operands
        frame_valid = positions < length
        normed = layer_norm(call_frames, ln_attn_gain).astype(jnp.bfloat16)
        packed = jnp.dot(normed, w_qkv, preferred_element_type=jnp.float32)
        queries = packed[:, :D].astype(jnp.bfloat16)
        keys_own = packed[:, D:2 * D].astype(jnp.bfloat16)
        values_own = packed[:, 2 * D:].astype(jnp.bfloat16)
        lead = jnp.zeros((LEFT, D), jnp.bfloat16)
        keys_pad = jnp.concatenate([lead, keys_own], axis=0)
        values_pad = jnp.concatenate([lead, values_own], axis=0)

        def block(block_index):
            block_first = (block_index * SPAN).astype(jnp.int32)
            query_block = lax.dynamic_slice_in_dim(queries, block_first, SPAN, 0)
            key_block = lax.dynamic_slice_in_dim(keys_pad, block_first, LEFT + SPAN, 0)
            value_block = lax.dynamic_slice_in_dim(values_pad, block_first, LEFT + SPAN, 0)
            key_pos = block_first - LEFT + jnp.arange(LEFT + SPAN, dtype=jnp.int32)
            query_pos = block_first + jnp.arange(SPAN, dtype=jnp.int32)
            allowed = (key_pos[None, :] >= 0) & ((key_pos[None, :] < length) | (key_pos[None, :] == query_pos[:, None]))
            query_heads = query_block.reshape(SPAN, HEADS, HEAD_DIM).astype(jnp.float32)
            key_heads = key_block.reshape(LEFT + SPAN, HEADS, HEAD_DIM).astype(jnp.float32)
            value_heads = value_block.reshape(LEFT + SPAN, HEADS, HEAD_DIM).astype(jnp.float32)
            scores = jnp.einsum('qhd,khd->hqk', query_heads, key_heads) / jnp.sqrt(jnp.float32(HEAD_DIM))
            raised = jnp.where(allowed[None], jnp.exp(scores), 0.0)
            probs = (raised / lax.optimization_barrier(jnp.sum(raised, axis=-1, keepdims=True))).astype(jnp.bfloat16)
            context = jnp.einsum('hqk,khd->qhd', probs.astype(jnp.float32), value_heads)
            return context.reshape(SPAN, D).astype(jnp.bfloat16)
        context = lax.map(block, jnp.arange(FRAMES // SPAN, dtype=jnp.int32)).reshape(FRAMES, D)
        projected = jnp.dot(context, w_out, preferred_element_type=jnp.float32)
        attended = jnp.where(frame_valid[:, None], call_frames.astype(jnp.float32) + projected, 0.0).astype(jnp.bfloat16)
        conv_in = layer_norm(attended, ln_conv_gain).astype(jnp.bfloat16)
        expanded = jnp.dot(conv_in, w_pw1, preferred_element_type=jnp.float32)
        gated = expanded[:, :D] * jax.nn.sigmoid(expanded[:, D:])
        gated = jnp.where(frame_valid[:, None], gated, 0.0).astype(jnp.bfloat16)
        return (attended, gated)
    attended, gated = lax.map(first_pass, (frames, lengths))

    def depthwise_of(gated_call):
        padded = jnp.pad(gated_call, ((half, half), (0, 0)))
        result = jnp.zeros((FRAMES, D), jnp.float32)
        for tap_index in range(KERNEL):
            result = result + padded[tap_index:tap_index + FRAMES].astype(jnp.float32) * dw_kernel[tap_index]
        return result

    def moments(operands):
        gated_call, length = operands
        depthwise = depthwise_of(gated_call)
        masked = jnp.where((positions < length)[:, None], depthwise, 0.0)
        return (lax.optimization_barrier(jnp.sum(masked, axis=0)), lax.optimization_barrier(jnp.sum(masked * depthwise, axis=0)))
    first_moment, second_moment = lax.map(moments, (gated, lengths))
    count_all = jnp.sum(lengths).astype(jnp.float32)
    average = lax.optimization_barrier(jnp.sum(first_moment, axis=0)) / count_all
    second = lax.optimization_barrier(jnp.sum(second_moment, axis=0)) / count_all

    def finish(operands):
        gated_call, length = operands
        depthwise = depthwise_of(gated_call)
        normal_act = (depthwise - average) * lax.rsqrt(second - average * average + 1e-05) * bn_gain + bn_bias
        activated = normal_act * jax.nn.sigmoid(normal_act)
        return jnp.where((positions < length)[:, None], activated, 0.0).astype(jnp.bfloat16)
    conv_act = lax.map(finish, (gated, lengths))
    return (attended, conv_act)
```

```python
import jax
import jax.numpy as jnp
import numpy as np
from jax import lax
from jax.sharding import Mesh
from jax.sharding import PartitionSpec as P

HEAD_DIM = 64
SPAN = 128
LEFT = 1024
KERNEL = 9
TM = ("x", "y", "core")


def passed_along(value, axis, steps):
    count = lax.axis_size(axis)
    first, last = (max(0, -steps), min(count, count - steps))
    return lax.ppermute(value, axis, [(source, source + steps) for source in range(first, last)])


def with_halo(cells, axis, width):
    count = lax.axis_size(axis)
    ends = count - 1
    head = lax.slice_in_dim(cells, 0, width, axis=0)
    tail = lax.slice_in_dim(cells, cells.shape[0] - width, cells.shape[0], axis=0)
    return jnp.concatenate(
        [
            lax.ppermute(tail, axis, [(i, (i + 1) % count) for i in range(ends)]),
            cells,
            lax.ppermute(head, axis, [((i + 1) % count, i) for i in range(ends)]),
        ],
        axis=0,
    )


def layer_norm(values, gain_vec):
    wide = values.astype(jnp.float32)
    center = wide - jnp.mean(wide, axis=-1, keepdims=True)
    spread = jnp.mean(center * center, axis=-1, keepdims=True)
    return center * lax.rsqrt(spread + 1e-05) * gain_vec


def contract_with(left, rows_piece):
    return jnp.dot(left, rows_piece, preferred_element_type=jnp.float32)


def on_device(
    frames, lengths, ln_attn_gain, w_qkv, w_out, ln_conv_gain, w_pw1, dw_kernel, bn_gain, bn_bias
):
    stream = frames[0]
    frame_count, model_width = stream.shape
    head_count = model_width // HEAD_DIM
    length = lax.dynamic_index_in_dim(lengths, lax.axis_index("call"), 0, keepdims=False)
    first_row = lax.axis_index(TM) * frame_count
    query_pos = first_row + jnp.arange(frame_count, dtype=jnp.int32)
    frame_valid = query_pos < length
    qkv_cols = w_qkv.shape[1]
    out_cols = w_out.shape[1]
    weights = lax.all_gather(
        jnp.concatenate([w_qkv, w_out, w_pw1], axis=1), TM, axis=0, tiled=True
    )
    prior_blocks = LEFT // frame_count
    blocks = []
    current = stream
    for hop_index in range(prior_blocks):
        current = passed_along(current, TM, 1)
        blocks.append(current)
    context_frames = jnp.concatenate(blocks[::-1] + [stream], axis=0)
    key_count = context_frames.shape[0]
    normed_all = layer_norm(context_frames, ln_attn_gain).astype(jnp.bfloat16)
    normed = normed_all[key_count - frame_count :]
    queries = contract_with(normed, weights[:, :model_width]).astype(jnp.bfloat16)
    key_value = contract_with(normed_all, weights[:, model_width:qkv_cols])
    keys = key_value[:, :model_width].astype(jnp.bfloat16)
    values = key_value[:, model_width:].astype(jnp.bfloat16)
    key_pos = first_row - prior_blocks * frame_count + jnp.arange(key_count, dtype=jnp.int32)
    span_first = query_pos // SPAN * SPAN
    allowed = (key_pos[None, :] >= 0) & (key_pos[None, :] >= span_first[:, None] - LEFT)
    allowed = allowed & (key_pos[None, :] < span_first[:, None] + SPAN)
    allowed = allowed & ((key_pos[None, :] < length) | (key_pos[None, :] == query_pos[:, None]))
    group_size = 4
    group_count = head_count // group_size
    query_groups = queries.reshape(frame_count, group_count, group_size, HEAD_DIM).transpose(
        1, 0, 2, 3
    )
    key_groups = keys.reshape(key_count, group_count, group_size, HEAD_DIM).transpose(1, 0, 2, 3)
    value_groups = values.reshape(key_count, group_count, group_size, HEAD_DIM).transpose(
        1, 0, 2, 3
    )
    scale_factor = 1.0 / jnp.sqrt(jnp.float32(HEAD_DIM))

    def attend_group(operands):
        query_part, key_part, value_part = operands
        scores = (
            jnp.einsum("qhd,khd->hqk", query_part, key_part, preferred_element_type=jnp.float32)
            * scale_factor
        )
        raised = jnp.where(allowed[None], jnp.exp(scores), 0.0)
        probs = (raised / jnp.sum(raised, axis=-1, keepdims=True)).astype(jnp.bfloat16)
        mixed = jnp.einsum("hqk,khd->qhd", probs, value_part, preferred_element_type=jnp.float32)
        return mixed.astype(jnp.bfloat16)

    context = lax.map(attend_group, (query_groups, key_groups, value_groups))
    context = context.transpose(1, 0, 2, 3).reshape(frame_count, model_width)
    projected = contract_with(context, weights[:, qkv_cols : qkv_cols + out_cols])
    attended = jnp.where(frame_valid[:, None], stream.astype(jnp.float32) + projected, 0.0).astype(
        jnp.bfloat16
    )
    conv_in = layer_norm(attended, ln_conv_gain).astype(jnp.bfloat16)
    expanded = contract_with(conv_in, weights[:, qkv_cols + out_cols :])
    gated = expanded[:, :model_width] * jax.nn.sigmoid(expanded[:, model_width:])
    gated = jnp.where(frame_valid[:, None], gated, 0.0).astype(jnp.bfloat16)
    padded = with_halo(gated, TM, KERNEL // 2)
    depthwise = jnp.zeros((frame_count, model_width), jnp.float32)
    for tap_index in range(KERNEL):
        depthwise = (
            depthwise
            + padded[tap_index : tap_index + frame_count].astype(jnp.float32) * dw_kernel[tap_index]
        )
    masked = jnp.where(frame_valid[:, None], depthwise, 0.0)
    moments = (jnp.sum(masked, axis=0), jnp.sum(masked * depthwise, axis=0))
    for axis in ("core", "y", "x", "call"):
        moments = lax.psum(moments, axis)
    first_moment, second_moment = moments
    count_all = jnp.sum(lengths).astype(jnp.float32)
    average = first_moment / count_all
    second = second_moment / count_all
    normal_act = (depthwise - average) * lax.rsqrt(
        second - average * average + 1e-05
    ) * bn_gain + bn_bias
    activated = normal_act * jax.nn.sigmoid(normal_act)
    conv_act = jnp.where(frame_valid[:, None], activated, 0.0).astype(jnp.bfloat16)
    return (attended[None], conv_act[None])


def physical_mesh(mesh):
    devices = mesh.devices
    calls, tms = devices.shape
    first = devices[0]
    xs = len({d.coords[0] for d in first})
    ys = len({d.coords[1] for d in first})
    cores = tms // (xs * ys)
    grid = np.array(
        [[(d.coords[0], d.coords[1], d.core_on_chip) for d in row] for row in devices]
    )
    expect = np.stack(
        np.meshgrid(np.arange(xs), np.arange(ys), np.arange(cores), indexing="ij"), -1
    ).reshape(-1, 3)
    grid = grid - grid[:, :1]
    assert (grid == expect[None]).all()
    return Mesh(devices.reshape(calls, xs, ys, cores), ("call",) + TM)


def solution(mesh):
    mesh4 = physical_mesh(mesh)
    rows = P(TM, None)
    stream = P("call", TM, None)
    return jax.shard_map(
        on_device,
        mesh=mesh4,
        in_specs=(stream, P(), P(), rows, rows, P(), rows, P(), P(), P()),
        out_specs=(stream, stream),
        check_vma=False,
    )
```

```python
import jax
import jax.numpy as jnp
import numpy as np
from jax import lax
from jax.sharding import Mesh
from jax.sharding import PartitionSpec as P

HEAD_DIM = 64
SPAN = 128
LEFT = 1024
KERNEL = 9
TM = ("x", "y", "core")


def passed_along(value, axis, steps):
    count = lax.axis_size(axis)
    first, last = (max(0, -steps), min(count, count - steps))
    return lax.ppermute(value, axis, [(source, source + steps) for source in range(first, last)])


def with_halo(cells, axis, width):
    count = lax.axis_size(axis)
    ends = count - 1
    head = lax.slice_in_dim(cells, 0, width, axis=0)
    tail = lax.slice_in_dim(cells, cells.shape[0] - width, cells.shape[0], axis=0)
    return jnp.concatenate(
        [
            lax.ppermute(tail, axis, [(i, (i + 1) % count) for i in range(ends)]),
            cells,
            lax.ppermute(head, axis, [((i + 1) % count, i) for i in range(ends)]),
        ],
        axis=0,
    )


def layer_norm(values, gain_vec):
    wide = values.astype(jnp.float32)
    center = wide - jnp.mean(wide, axis=-1, keepdims=True)
    spread = jnp.mean(center * center, axis=-1, keepdims=True)
    return center * lax.rsqrt(spread + 1e-05) * gain_vec


def contract_with(left, rows_piece):
    return jnp.dot(left, rows_piece, preferred_element_type=jnp.float32)


def on_device(
    frames, lengths, ln_attn_gain, w_qkv, w_out, ln_conv_gain, w_pw1, dw_kernel, bn_gain, bn_bias
):
    stream = frames[0]
    frame_count, model_width = stream.shape
    head_count = model_width // HEAD_DIM
    length = lax.dynamic_index_in_dim(lengths, lax.axis_index("call"), 0, keepdims=False)
    first_row = lax.axis_index(TM) * frame_count
    query_pos = first_row + jnp.arange(frame_count, dtype=jnp.int32)
    frame_valid = query_pos < length
    qkv_cols = w_qkv.shape[1]
    out_cols = w_out.shape[1]
    weights = lax.all_gather(
        jnp.concatenate([w_qkv, w_out, w_pw1], axis=1), TM, axis=0, tiled=True
    )
    prior_blocks = LEFT // frame_count
    blocks = []
    current = stream
    for hop_index in range(prior_blocks):
        current = passed_along(current, TM, 1)
        blocks.append(current)
    context_frames = jnp.concatenate(blocks[::-1] + [stream], axis=0)
    key_count = context_frames.shape[0]
    normed_all = layer_norm(context_frames, ln_attn_gain).astype(jnp.bfloat16)
    normed = normed_all[key_count - frame_count :]
    queries = contract_with(normed, weights[:, :model_width]).astype(jnp.bfloat16)
    key_value = contract_with(normed_all, weights[:, model_width:qkv_cols])
    keys = key_value[:, :model_width].astype(jnp.bfloat16)
    values = key_value[:, model_width:].astype(jnp.bfloat16)
    key_pos = first_row - prior_blocks * frame_count + jnp.arange(key_count, dtype=jnp.int32)
    span_first = query_pos // SPAN * SPAN
    allowed = (key_pos[None, :] >= 0) & (key_pos[None, :] >= span_first[:, None] - LEFT)
    allowed = allowed & (key_pos[None, :] < span_first[:, None] + SPAN)
    allowed = allowed & ((key_pos[None, :] < length) | (key_pos[None, :] == query_pos[:, None]))
    group_size = 4
    group_count = head_count // group_size
    query_groups = queries.reshape(frame_count, group_count, group_size, HEAD_DIM).transpose(
        1, 0, 2, 3
    )
    key_groups = keys.reshape(key_count, group_count, group_size, HEAD_DIM).transpose(1, 0, 2, 3)
    value_groups = values.reshape(key_count, group_count, group_size, HEAD_DIM).transpose(
        1, 0, 2, 3
    )
    scale_factor = 1.0 / jnp.sqrt(jnp.float32(HEAD_DIM))

    def attend_group(operands):
        query_part, key_part, value_part = operands
        scores = (
            jnp.einsum("qhd,khd->hqk", query_part, key_part, preferred_element_type=jnp.float32)
            * scale_factor
        )
        raised = jnp.where(allowed[None], jnp.exp(scores), 0.0)
        probs = (raised / jnp.sum(raised, axis=-1, keepdims=True)).astype(jnp.bfloat16)
        mixed = jnp.einsum("hqk,khd->qhd", probs, value_part, preferred_element_type=jnp.float32)
        return mixed.astype(jnp.bfloat16)

    context = lax.map(attend_group, (query_groups, key_groups, value_groups))
    context = context.transpose(1, 0, 2, 3).reshape(frame_count, model_width)
    projected = contract_with(context, weights[:, qkv_cols : qkv_cols + out_cols])
    attended = jnp.where(frame_valid[:, None], stream.astype(jnp.float32) + projected, 0.0).astype(
        jnp.bfloat16
    )
    conv_in = layer_norm(attended, ln_conv_gain).astype(jnp.bfloat16)
    expanded = contract_with(conv_in, weights[:, qkv_cols + out_cols :])
    gated = expanded[:, :model_width] * jax.nn.sigmoid(expanded[:, model_width:])
    gated = jnp.where(frame_valid[:, None], gated, 0.0).astype(jnp.bfloat16)
    padded = with_halo(gated, TM, KERNEL // 2)
    depthwise = jnp.zeros((frame_count, model_width), jnp.float32)
    for tap_index in range(KERNEL):
        depthwise = (
            depthwise
            + padded[tap_index : tap_index + frame_count].astype(jnp.float32) * dw_kernel[tap_index]
        )
    masked = jnp.where(frame_valid[:, None], depthwise, 0.0)
    moments = (jnp.sum(masked, axis=0), jnp.sum(masked * depthwise, axis=0))
    moments = jnp.stack(moments)
    for axis in ("core", "y", "x", "call"):
        moments = jnp.sum(lax.all_gather(moments, axis), axis=0)
    first_moment, second_moment = moments[0], moments[1]
    count_all = jnp.sum(lengths).astype(jnp.float32)
    average = first_moment / count_all
    second = second_moment / count_all
    normal_act = (depthwise - average) * lax.rsqrt(
        second - average * average + 1e-05
    ) * bn_gain + bn_bias
    activated = normal_act * jax.nn.sigmoid(normal_act)
    conv_act = jnp.where(frame_valid[:, None], activated, 0.0).astype(jnp.bfloat16)
    return (attended[None], conv_act[None])


def physical_mesh(mesh):
    devices = mesh.devices
    calls, tms = devices.shape
    first = devices[0]
    xs = len({d.coords[0] for d in first})
    ys = len({d.coords[1] for d in first})
    cores = tms // (xs * ys)
    grid = np.array(
        [[(d.coords[0], d.coords[1], d.core_on_chip) for d in row] for row in devices]
    )
    expect = np.stack(
        np.meshgrid(np.arange(xs), np.arange(ys), np.arange(cores), indexing="ij"), -1
    ).reshape(-1, 3)
    grid = grid - grid[:, :1]
    assert (grid == expect[None]).all()
    return Mesh(devices.reshape(calls, xs, ys, cores), ("call",) + TM)


def solution(mesh):
    mesh4 = physical_mesh(mesh)
    rows = P(TM, None)
    stream = P("call", TM, None)
    return jax.shard_map(
        on_device,
        mesh=mesh4,
        in_specs=(stream, P(), P(), rows, rows, P(), rows, P(), P(), P()),
        out_specs=(stream, stream),
        check_vma=False,
    )
```

```python
import jax
import jax.numpy as jnp
import numpy as np
from jax import lax
from jax.sharding import Mesh
from jax.sharding import PartitionSpec as P

HEAD_DIM = 64
SPAN = 128
LEFT = 1024
KERNEL = 9
TM = ("x", "y", "core")


def passed_along(value, axis, steps):
    count = lax.axis_size(axis)
    first, last = (max(0, -steps), min(count, count - steps))
    return lax.ppermute(value, axis, [(source, source + steps) for source in range(first, last)])


def with_halo(cells, axis, width):
    count = lax.axis_size(axis)
    ends = count - 1
    head = lax.slice_in_dim(cells, 0, width, axis=0)
    tail = lax.slice_in_dim(cells, cells.shape[0] - width, cells.shape[0], axis=0)
    return jnp.concatenate(
        [
            lax.ppermute(tail, axis, [(i, (i + 1) % count) for i in range(ends)]),
            cells,
            lax.ppermute(head, axis, [((i + 1) % count, i) for i in range(ends)]),
        ],
        axis=0,
    )


def layer_norm(values, gain_vec):
    wide = values.astype(jnp.float32)
    center = wide - jnp.mean(wide, axis=-1, keepdims=True)
    spread = jnp.mean(center * center, axis=-1, keepdims=True)
    return center * lax.rsqrt(spread + 1e-05) * gain_vec


def contract_with(left, rows_piece):
    return jnp.dot(left, rows_piece, preferred_element_type=jnp.float32)


def on_device(
    frames, lengths, ln_attn_gain, w_qkv, w_out, ln_conv_gain, w_pw1, dw_kernel, bn_gain, bn_bias
):
    stream = frames[0]
    frame_count, model_width = stream.shape
    head_count = model_width // HEAD_DIM
    length = lax.dynamic_index_in_dim(lengths, lax.axis_index("call"), 0, keepdims=False)
    first_row = lax.axis_index(TM) * frame_count
    query_pos = first_row + jnp.arange(frame_count, dtype=jnp.int32)
    frame_valid = query_pos < length
    qkv_cols = w_qkv.shape[1]
    out_cols = w_out.shape[1]
    core = lax.axis_index("core")
    cores = lax.axis_size("core")
    swap = [(0, 1), (1, 0)]
    packed = jnp.concatenate([w_qkv, w_out, w_pw1], axis=1)
    half = packed.shape[1] // 2
    halves = (packed[:, :half], packed[:, half:])
    given = lax.ppermute(jnp.where(core == 0, halves[1], halves[0]), "core", swap)
    kept = jnp.where(core == 0, halves[0], halves[1])
    pair = jnp.where(core == 0, jnp.stack([kept, given]), jnp.stack([given, kept]))
    gathered = lax.all_gather(pair.reshape(-1, half), ("x", "y"), axis=0, tiled=True)
    prior_blocks = LEFT // frame_count
    chip_hops = prior_blocks // cores
    blocks = [stream]
    current = stream
    for hop_index in range(chip_hops):
        current = passed_along(current, ("x", "y"), 1)
        blocks.append(current)
    mine = jnp.stack(blocks[::-1])
    gathered, mine = lax.optimization_barrier((gathered, mine))
    other = lax.ppermute(gathered, "core", swap)
    weights = jnp.where(
        core == 0,
        jnp.concatenate([gathered, other], axis=1),
        jnp.concatenate([other, gathered], axis=1),
    )
    theirs = lax.ppermute(mine, "core", swap)
    by_chip = jnp.where(core == 0, jnp.stack([mine, theirs], 1), jnp.stack([theirs, mine], 1))
    by_chip = by_chip.reshape(-1, model_width)
    context_frames = lax.dynamic_slice_in_dim(
        by_chip, core * frame_count, (prior_blocks + 1) * frame_count, 0
    )
    key_count = context_frames.shape[0]
    normed_all = layer_norm(context_frames, ln_attn_gain).astype(jnp.bfloat16)
    normed = normed_all[key_count - frame_count :]
    queries = contract_with(normed, weights[:, :model_width]).astype(jnp.bfloat16)
    key_value = contract_with(normed_all, weights[:, model_width:qkv_cols])
    keys = key_value[:, :model_width].astype(jnp.bfloat16)
    values = key_value[:, model_width:].astype(jnp.bfloat16)
    key_pos = first_row - prior_blocks * frame_count + jnp.arange(key_count, dtype=jnp.int32)
    span_first = query_pos // SPAN * SPAN
    allowed = (key_pos[None, :] >= 0) & (key_pos[None, :] >= span_first[:, None] - LEFT)
    allowed = allowed & (key_pos[None, :] < span_first[:, None] + SPAN)
    allowed = allowed & ((key_pos[None, :] < length) | (key_pos[None, :] == query_pos[:, None]))
    group_size = 4
    group_count = head_count // group_size
    query_groups = queries.reshape(frame_count, group_count, group_size, HEAD_DIM).transpose(
        1, 0, 2, 3
    )
    key_groups = keys.reshape(key_count, group_count, group_size, HEAD_DIM).transpose(1, 0, 2, 3)
    value_groups = values.reshape(key_count, group_count, group_size, HEAD_DIM).transpose(
        1, 0, 2, 3
    )
    scale_factor = 1.0 / jnp.sqrt(jnp.float32(HEAD_DIM))

    def attend_group(operands):
        query_part, key_part, value_part = operands
        scores = (
            jnp.einsum("qhd,khd->hqk", query_part, key_part, preferred_element_type=jnp.float32)
            * scale_factor
        )
        raised = jnp.where(allowed[None], jnp.exp(scores), 0.0)
        probs = (raised / jnp.sum(raised, axis=-1, keepdims=True)).astype(jnp.bfloat16)
        mixed = jnp.einsum("hqk,khd->qhd", probs, value_part, preferred_element_type=jnp.float32)
        return mixed.astype(jnp.bfloat16)

    context = lax.map(attend_group, (query_groups, key_groups, value_groups))
    context = context.transpose(1, 0, 2, 3).reshape(frame_count, model_width)
    projected = contract_with(context, weights[:, qkv_cols : qkv_cols + out_cols])
    attended = jnp.where(frame_valid[:, None], stream.astype(jnp.float32) + projected, 0.0).astype(
        jnp.bfloat16
    )
    conv_in = layer_norm(attended, ln_conv_gain).astype(jnp.bfloat16)
    expanded = contract_with(conv_in, weights[:, qkv_cols + out_cols :])
    gated = expanded[:, :model_width] * jax.nn.sigmoid(expanded[:, model_width:])
    gated = jnp.where(frame_valid[:, None], gated, 0.0).astype(jnp.bfloat16)
    padded = with_halo(gated, TM, KERNEL // 2)
    depthwise = jnp.zeros((frame_count, model_width), jnp.float32)
    for tap_index in range(KERNEL):
        depthwise = (
            depthwise
            + padded[tap_index : tap_index + frame_count].astype(jnp.float32) * dw_kernel[tap_index]
        )
    masked = jnp.where(frame_valid[:, None], depthwise, 0.0)
    moments = (jnp.sum(masked, axis=0), jnp.sum(masked * depthwise, axis=0))
    for axis in ("core", "y", "x", "call"):
        moments = lax.psum(moments, axis)
    first_moment, second_moment = moments
    count_all = jnp.sum(lengths).astype(jnp.float32)
    average = first_moment / count_all
    second = second_moment / count_all
    normal_act = (depthwise - average) * lax.rsqrt(
        second - average * average + 1e-05
    ) * bn_gain + bn_bias
    activated = normal_act * jax.nn.sigmoid(normal_act)
    conv_act = jnp.where(frame_valid[:, None], activated, 0.0).astype(jnp.bfloat16)
    return (attended[None], conv_act[None])


def physical_mesh(mesh):
    devices = mesh.devices
    calls, tms = devices.shape
    first = devices[0]
    xs = len({d.coords[0] for d in first})
    ys = len({d.coords[1] for d in first})
    cores = tms // (xs * ys)
    grid = np.array(
        [[(d.coords[0], d.coords[1], d.core_on_chip) for d in row] for row in devices]
    )
    expect = np.stack(
        np.meshgrid(np.arange(xs), np.arange(ys), np.arange(cores), indexing="ij"), -1
    ).reshape(-1, 3)
    grid = grid - grid[:, :1]
    assert (grid == expect[None]).all()
    return Mesh(devices.reshape(calls, xs, ys, cores), ("call",) + TM)


def solution(mesh):
    mesh4 = physical_mesh(mesh)
    rows = P(TM, None)
    stream = P("call", TM, None)
    return jax.shard_map(
        on_device,
        mesh=mesh4,
        in_specs=(stream, P(), P(), rows, rows, P(), rows, P(), P(), P()),
        out_specs=(stream, stream),
        check_vma=False,
    )
```

```python
import jax
import jax.numpy as jnp
import numpy as np
from jax import lax
from jax.sharding import Mesh
from jax.sharding import PartitionSpec as P

HEAD_DIM = 64
SPAN = 128
LEFT = 1024
KERNEL = 9
TM = ("x", "y", "core")


def passed_along(value, axis, steps):
    count = lax.axis_size(axis)
    first, last = (max(0, -steps), min(count, count - steps))
    return lax.ppermute(value, axis, [(source, source + steps) for source in range(first, last)])


def with_halo(cells, axis, width):
    count = lax.axis_size(axis)
    ends = count - 1
    head = lax.slice_in_dim(cells, 0, width, axis=0)
    tail = lax.slice_in_dim(cells, cells.shape[0] - width, cells.shape[0], axis=0)
    return jnp.concatenate(
        [
            lax.ppermute(tail, axis, [(i, (i + 1) % count) for i in range(ends)]),
            cells,
            lax.ppermute(head, axis, [((i + 1) % count, i) for i in range(ends)]),
        ],
        axis=0,
    )


def layer_norm(values, gain_vec):
    wide = values.astype(jnp.float32)
    center = wide - jnp.mean(wide, axis=-1, keepdims=True)
    spread = jnp.mean(center * center, axis=-1, keepdims=True)
    return center * lax.rsqrt(spread + 1e-05) * gain_vec


def contract_with(left, rows_piece):
    return jnp.dot(left, rows_piece, preferred_element_type=jnp.float32)


def on_device(
    frames, lengths, ln_attn_gain, w_qkv, w_out, ln_conv_gain, w_pw1, dw_kernel, bn_gain, bn_bias
):
    stream = frames[0]
    frame_count, model_width = stream.shape
    head_count = model_width // HEAD_DIM
    length = lax.dynamic_index_in_dim(lengths, lax.axis_index("call"), 0, keepdims=False)
    first_row = lax.axis_index(TM) * frame_count
    query_pos = first_row + jnp.arange(frame_count, dtype=jnp.int32)
    frame_valid = query_pos < length
    qkv_cols = w_qkv.shape[1]
    out_cols = w_out.shape[1]
    weights = lax.all_gather(
        jnp.concatenate([w_qkv, w_out, w_pw1], axis=1), TM, axis=0, tiled=True
    )
    prior_blocks = LEFT // frame_count
    blocks = []
    current = stream
    for hop_index in range(prior_blocks):
        current = passed_along(current, TM, 1)
        blocks.append(current)
    context_frames = jnp.concatenate(blocks[::-1] + [stream], axis=0)
    key_count = context_frames.shape[0]
    normed_all = layer_norm(context_frames, ln_attn_gain).astype(jnp.bfloat16)
    normed = normed_all[key_count - frame_count :]
    queries = contract_with(normed, weights[:, :model_width]).astype(jnp.bfloat16)
    key_value = contract_with(normed_all, weights[:, model_width:qkv_cols])
    keys = key_value[:, :model_width].astype(jnp.bfloat16)
    values = key_value[:, model_width:].astype(jnp.bfloat16)
    key_pos = first_row - prior_blocks * frame_count + jnp.arange(key_count, dtype=jnp.int32)
    span_first = query_pos // SPAN * SPAN
    allowed = (key_pos[None, :] >= 0) & (key_pos[None, :] >= span_first[:, None] - LEFT)
    allowed = allowed & (key_pos[None, :] < span_first[:, None] + SPAN)
    allowed = allowed & ((key_pos[None, :] < length) | (key_pos[None, :] == query_pos[:, None]))
    query_heads = queries.reshape(frame_count, head_count, HEAD_DIM)
    key_heads = keys.reshape(key_count, head_count, HEAD_DIM)
    value_heads = values.reshape(key_count, head_count, HEAD_DIM)
    scale_factor = 1.0 / jnp.sqrt(jnp.float32(HEAD_DIM))
    scores = (
        jnp.einsum("qhd,khd->hqk", query_heads, key_heads, preferred_element_type=jnp.float32)
        * scale_factor
    )
    raised = jnp.where(allowed[None], jnp.exp(scores), 0.0)
    probs = (raised / jnp.sum(raised, axis=-1, keepdims=True)).astype(jnp.bfloat16)
    context = jnp.einsum("hqk,khd->qhd", probs, value_heads, preferred_element_type=jnp.float32)
    context = context.astype(jnp.bfloat16).reshape(frame_count, model_width)
    projected = contract_with(context, weights[:, qkv_cols : qkv_cols + out_cols])
    attended = jnp.where(frame_valid[:, None], stream.astype(jnp.float32) + projected, 0.0).astype(
        jnp.bfloat16
    )
    conv_in = layer_norm(attended, ln_conv_gain).astype(jnp.bfloat16)
    expanded = contract_with(conv_in, weights[:, qkv_cols + out_cols :])
    gated = expanded[:, :model_width] * jax.nn.sigmoid(expanded[:, model_width:])
    gated = jnp.where(frame_valid[:, None], gated, 0.0).astype(jnp.bfloat16)
    padded = with_halo(gated, TM, KERNEL // 2)
    depthwise = jnp.zeros((frame_count, model_width), jnp.float32)
    for tap_index in range(KERNEL):
        depthwise = (
            depthwise
            + padded[tap_index : tap_index + frame_count].astype(jnp.float32) * dw_kernel[tap_index]
        )
    masked = jnp.where(frame_valid[:, None], depthwise, 0.0)
    moments = (jnp.sum(masked, axis=0), jnp.sum(masked * depthwise, axis=0))
    for axis in ("core", "y", "x", "call"):
        moments = lax.psum(moments, axis)
    first_moment, second_moment = moments
    count_all = jnp.sum(lengths).astype(jnp.float32)
    average = first_moment / count_all
    second = second_moment / count_all
    normal_act = (depthwise - average) * lax.rsqrt(
        second - average * average + 1e-05
    ) * bn_gain + bn_bias
    activated = normal_act * jax.nn.sigmoid(normal_act)
    conv_act = jnp.where(frame_valid[:, None], activated, 0.0).astype(jnp.bfloat16)
    return (attended[None], conv_act[None])


def physical_mesh(mesh):
    devices = mesh.devices
    calls, tms = devices.shape
    first = devices[0]
    xs = len({d.coords[0] for d in first})
    ys = len({d.coords[1] for d in first})
    cores = tms // (xs * ys)
    grid = np.array(
        [[(d.coords[0], d.coords[1], d.core_on_chip) for d in row] for row in devices]
    )
    expect = np.stack(
        np.meshgrid(np.arange(xs), np.arange(ys), np.arange(cores), indexing="ij"), -1
    ).reshape(-1, 3)
    grid = grid - grid[:, :1]
    assert (grid == expect[None]).all()
    return Mesh(devices.reshape(calls, xs, ys, cores), ("call",) + TM)


def solution(mesh):
    mesh4 = physical_mesh(mesh)
    rows = P(TM, None)
    stream = P("call", TM, None)
    return jax.shard_map(
        on_device,
        mesh=mesh4,
        in_specs=(stream, P(), P(), rows, rows, P(), rows, P(), P(), P()),
        out_specs=(stream, stream),
        check_vma=False,
    )
```

```python
import jax
import jax.numpy as jnp
import numpy as np
from jax import lax
from jax.sharding import Mesh
from jax.sharding import PartitionSpec as P

HEAD_DIM = 64
SPAN = 128
LEFT = 1024
KERNEL = 9
TM = ("x", "y", "core")


def passed_along(value, axis, steps):
    count = lax.axis_size(axis)
    first, last = (max(0, -steps), min(count, count - steps))
    return lax.ppermute(value, axis, [(source, source + steps) for source in range(first, last)])


def with_halo(cells, axis, width):
    count = lax.axis_size(axis)
    ends = count - 1
    head = lax.slice_in_dim(cells, 0, width, axis=0)
    tail = lax.slice_in_dim(cells, cells.shape[0] - width, cells.shape[0], axis=0)
    return jnp.concatenate(
        [
            lax.ppermute(tail, axis, [(i, (i + 1) % count) for i in range(ends)]),
            cells,
            lax.ppermute(head, axis, [((i + 1) % count, i) for i in range(ends)]),
        ],
        axis=0,
    )


def layer_norm(values, gain_vec):
    wide = values.astype(jnp.float32)
    center = wide - jnp.mean(wide, axis=-1, keepdims=True)
    spread = jnp.mean(center * center, axis=-1, keepdims=True)
    return center * lax.rsqrt(spread + 1e-05) * gain_vec


def contract_with(left, rows_piece):
    return jnp.dot(left, rows_piece, preferred_element_type=jnp.float32)


def on_device(
    frames, lengths, ln_attn_gain, w_qkv, w_out, ln_conv_gain, w_pw1, dw_kernel, bn_gain, bn_bias
):
    stream = frames[0]
    frame_count, model_width = stream.shape
    head_count = model_width // HEAD_DIM
    length = lax.dynamic_index_in_dim(lengths, lax.axis_index("call"), 0, keepdims=False)
    first_row = lax.axis_index(TM) * frame_count
    query_pos = first_row + jnp.arange(frame_count, dtype=jnp.int32)
    frame_valid = query_pos < length
    qkv_cols = w_qkv.shape[1]
    out_cols = w_out.shape[1]
    weights = lax.all_gather(
        jnp.concatenate([w_qkv, w_out, w_pw1], axis=1), TM, axis=0, tiled=True
    )
    prior_blocks = LEFT // frame_count
    blocks = []
    current = stream
    for hop_index in range(prior_blocks):
        current = passed_along(current, TM, 1)
        blocks.append(current)
    context_frames = jnp.concatenate(blocks[::-1] + [stream], axis=0)
    key_count = context_frames.shape[0]
    normed_all = layer_norm(context_frames, ln_attn_gain).astype(jnp.bfloat16)
    normed = normed_all[key_count - frame_count :]
    queries = contract_with(normed, weights[:, :model_width]).astype(jnp.bfloat16)
    key_value = contract_with(normed_all, weights[:, model_width:qkv_cols])
    keys = key_value[:, :model_width].astype(jnp.bfloat16)
    values = key_value[:, model_width:].astype(jnp.bfloat16)
    key_pos = first_row - prior_blocks * frame_count + jnp.arange(key_count, dtype=jnp.int32)
    span_first = query_pos // SPAN * SPAN
    allowed = (key_pos[None, :] >= 0) & (key_pos[None, :] >= span_first[:, None] - LEFT)
    allowed = allowed & (key_pos[None, :] < span_first[:, None] + SPAN)
    allowed = allowed & ((key_pos[None, :] < length) | (key_pos[None, :] == query_pos[:, None]))
    query_heads = queries.reshape(frame_count, head_count, HEAD_DIM)
    key_heads = keys.reshape(key_count, head_count, HEAD_DIM)
    value_heads = values.reshape(key_count, head_count, HEAD_DIM)
    scale_factor = 1.0 / jnp.sqrt(jnp.float32(HEAD_DIM))
    scores = (
        jnp.einsum("qhd,khd->hqk", query_heads, key_heads, preferred_element_type=jnp.float32)
        * scale_factor
    )
    raised = jnp.where(allowed[None], jnp.exp(scores), 0.0)
    probs = (raised / jnp.sum(raised, axis=-1, keepdims=True)).astype(jnp.bfloat16)
    context = jnp.einsum("hqk,khd->qhd", probs, value_heads, preferred_element_type=jnp.float32)
    context = context.astype(jnp.bfloat16).reshape(frame_count, model_width)
    projected = contract_with(context, weights[:, qkv_cols : qkv_cols + out_cols])
    attended = jnp.where(frame_valid[:, None], stream.astype(jnp.float32) + projected, 0.0).astype(
        jnp.bfloat16
    )
    conv_in = layer_norm(attended, ln_conv_gain).astype(jnp.bfloat16)
    expanded = contract_with(conv_in, weights[:, qkv_cols + out_cols :])
    gated = expanded[:, :model_width] * jax.nn.sigmoid(expanded[:, model_width:])
    gated = jnp.where(frame_valid[:, None], gated, 0.0).astype(jnp.bfloat16)
    padded = with_halo(gated, TM, KERNEL // 2)
    depthwise = jnp.zeros((frame_count, model_width), jnp.float32)
    for tap_index in range(KERNEL):
        depthwise = (
            depthwise
            + padded[tap_index : tap_index + frame_count].astype(jnp.float32) * dw_kernel[tap_index]
        )
    masked = jnp.where(frame_valid[:, None], depthwise, 0.0)
    moments = (jnp.sum(masked, axis=0), jnp.sum(masked * depthwise, axis=0))
    moments = jnp.stack(moments)
    for axis in ("core", "y", "x", "call"):
        count = lax.axis_size(axis)
        assert count & (count - 1) == 0
        stride = 1
        while stride < count:
            moments = moments + lax.ppermute(
                moments, axis, [(i, (i + stride) % count) for i in range(count)]
            )
            stride *= 2
    first_moment, second_moment = moments[0], moments[1]
    count_all = jnp.sum(lengths).astype(jnp.float32)
    average = first_moment / count_all
    second = second_moment / count_all
    normal_act = (depthwise - average) * lax.rsqrt(
        second - average * average + 1e-05
    ) * bn_gain + bn_bias
    activated = normal_act * jax.nn.sigmoid(normal_act)
    conv_act = jnp.where(frame_valid[:, None], activated, 0.0).astype(jnp.bfloat16)
    return (attended[None], conv_act[None])


def physical_mesh(mesh):
    devices = mesh.devices
    calls, tms = devices.shape
    first = devices[0]
    xs = len({d.coords[0] for d in first})
    ys = len({d.coords[1] for d in first})
    cores = tms // (xs * ys)
    grid = np.array(
        [[(d.coords[0], d.coords[1], d.core_on_chip) for d in row] for row in devices]
    )
    expect = np.stack(
        np.meshgrid(np.arange(xs), np.arange(ys), np.arange(cores), indexing="ij"), -1
    ).reshape(-1, 3)
    grid = grid - grid[:, :1]
    assert (grid == expect[None]).all()
    return Mesh(devices.reshape(calls, xs, ys, cores), ("call",) + TM)


def solution(mesh):
    mesh4 = physical_mesh(mesh)
    rows = P(TM, None)
    stream = P("call", TM, None)
    return jax.shard_map(
        on_device,
        mesh=mesh4,
        in_specs=(stream, P(), P(), rows, rows, P(), rows, P(), P(), P()),
        out_specs=(stream, stream),
        check_vma=False,
    )
```

```python
import jax
import jax.numpy as jnp
import numpy as np
from jax import lax
from jax.sharding import Mesh
from jax.sharding import PartitionSpec as P

HEAD_DIM = 64
SPAN = 128
LEFT = 1024
KERNEL = 9
TM = ("x", "y", "core")


def passed_along(value, axis, steps):
    count = lax.axis_size(axis)
    first, last = (max(0, -steps), min(count, count - steps))
    return lax.ppermute(value, axis, [(source, source + steps) for source in range(first, last)])


def with_halo(cells, axis, width):
    count = lax.axis_size(axis)
    ends = count - 1
    head = lax.slice_in_dim(cells, 0, width, axis=0)
    tail = lax.slice_in_dim(cells, cells.shape[0] - width, cells.shape[0], axis=0)
    return jnp.concatenate(
        [
            lax.ppermute(tail, axis, [(i, (i + 1) % count) for i in range(ends)]),
            cells,
            lax.ppermute(head, axis, [((i + 1) % count, i) for i in range(ends)]),
        ],
        axis=0,
    )


def layer_norm(values, gain_vec):
    wide = values.astype(jnp.float32)
    center = wide - jnp.mean(wide, axis=-1, keepdims=True)
    spread = jnp.mean(center * center, axis=-1, keepdims=True)
    return center * lax.rsqrt(spread + 1e-05) * gain_vec


def contract_with(left, rows_piece):
    return jnp.dot(left, rows_piece, preferred_element_type=jnp.float32)


def on_device(
    frames, lengths, ln_attn_gain, w_qkv, w_out, ln_conv_gain, w_pw1, dw_kernel, bn_gain, bn_bias
):
    stream = frames[0]
    frame_count, model_width = stream.shape
    head_count = model_width // HEAD_DIM
    length = lax.dynamic_index_in_dim(lengths, lax.axis_index("call"), 0, keepdims=False)
    first_row = lax.axis_index(TM) * frame_count
    query_pos = first_row + jnp.arange(frame_count, dtype=jnp.int32)
    frame_valid = query_pos < length
    qkv_cols = w_qkv.shape[1]
    out_cols = w_out.shape[1]
    weights = lax.all_gather(
        jnp.concatenate([w_qkv, w_out, w_pw1], axis=1), TM, axis=0, tiled=True
    )
    prior_blocks = LEFT // frame_count
    blocks = []
    current = stream
    for hop_index in range(prior_blocks):
        current = passed_along(current, TM, 1)
        blocks.append(current)
    context_frames = jnp.concatenate(blocks[::-1] + [stream], axis=0)
    key_count = context_frames.shape[0]
    normed_all = layer_norm(context_frames, ln_attn_gain).astype(jnp.bfloat16)
    normed = normed_all[key_count - frame_count :]
    def heads_of(rows, columns):
        piece = weights[:, columns : columns + model_width].reshape(model_width, head_count, HEAD_DIM)
        return jnp.einsum(
            "kc,chd->hkd", rows, piece, preferred_element_type=jnp.float32
        ).astype(jnp.bfloat16)

    query_heads = heads_of(normed, 0)
    key_heads = heads_of(normed_all, model_width)
    value_heads = heads_of(normed_all, 2 * model_width)
    key_pos = first_row - prior_blocks * frame_count + jnp.arange(key_count, dtype=jnp.int32)
    span_first = query_pos // SPAN * SPAN
    allowed = (key_pos[None, :] >= 0) & (key_pos[None, :] >= span_first[:, None] - LEFT)
    allowed = allowed & (key_pos[None, :] < span_first[:, None] + SPAN)
    allowed = allowed & ((key_pos[None, :] < length) | (key_pos[None, :] == query_pos[:, None]))
    scale_factor = 1.0 / jnp.sqrt(jnp.float32(HEAD_DIM))
    scores = (
        jnp.einsum("hqd,hkd->hqk", query_heads, key_heads, preferred_element_type=jnp.float32)
        * scale_factor
    )
    raised = jnp.where(allowed[None], jnp.exp(scores), 0.0)
    probs = (raised / jnp.sum(raised, axis=-1, keepdims=True)).astype(jnp.bfloat16)
    context = jnp.einsum("hqk,hkd->hqd", probs, value_heads, preferred_element_type=jnp.float32)
    context = context.astype(jnp.bfloat16)
    out_piece = weights[:, qkv_cols : qkv_cols + out_cols].reshape(head_count, HEAD_DIM, out_cols)
    projected = jnp.einsum("hqd,hdo->qo", context, out_piece, preferred_element_type=jnp.float32)
    attended = jnp.where(frame_valid[:, None], stream.astype(jnp.float32) + projected, 0.0).astype(
        jnp.bfloat16
    )
    conv_in = layer_norm(attended, ln_conv_gain).astype(jnp.bfloat16)
    expanded = contract_with(conv_in, weights[:, qkv_cols + out_cols :])
    gated = expanded[:, :model_width] * jax.nn.sigmoid(expanded[:, model_width:])
    gated = jnp.where(frame_valid[:, None], gated, 0.0).astype(jnp.bfloat16)
    padded = with_halo(gated, TM, KERNEL // 2)
    depthwise = jnp.zeros((frame_count, model_width), jnp.float32)
    for tap_index in range(KERNEL):
        depthwise = (
            depthwise
            + padded[tap_index : tap_index + frame_count].astype(jnp.float32) * dw_kernel[tap_index]
        )
    masked = jnp.where(frame_valid[:, None], depthwise, 0.0)
    moments = (jnp.sum(masked, axis=0), jnp.sum(masked * depthwise, axis=0))
    for axis in ("core", "y", "x", "call"):
        moments = lax.psum(moments, axis)
    first_moment, second_moment = moments
    count_all = jnp.sum(lengths).astype(jnp.float32)
    average = first_moment / count_all
    second = second_moment / count_all
    normal_act = (depthwise - average) * lax.rsqrt(
        second - average * average + 1e-05
    ) * bn_gain + bn_bias
    activated = normal_act * jax.nn.sigmoid(normal_act)
    conv_act = jnp.where(frame_valid[:, None], activated, 0.0).astype(jnp.bfloat16)
    return (attended[None], conv_act[None])


def physical_mesh(mesh):
    devices = mesh.devices
    calls, tms = devices.shape
    first = devices[0]
    xs = len({d.coords[0] for d in first})
    ys = len({d.coords[1] for d in first})
    cores = tms // (xs * ys)
    grid = np.array(
        [[(d.coords[0], d.coords[1], d.core_on_chip) for d in row] for row in devices]
    )
    expect = np.stack(
        np.meshgrid(np.arange(xs), np.arange(ys), np.arange(cores), indexing="ij"), -1
    ).reshape(-1, 3)
    grid = grid - grid[:, :1]
    assert (grid == expect[None]).all()
    return Mesh(devices.reshape(calls, xs, ys, cores), ("call",) + TM)


def solution(mesh):
    mesh4 = physical_mesh(mesh)
    rows = P(TM, None)
    stream = P("call", TM, None)
    return jax.shard_map(
        on_device,
        mesh=mesh4,
        in_specs=(stream, P(), P(), rows, rows, P(), rows, P(), P(), P()),
        out_specs=(stream, stream),
        check_vma=False,
    )
```

```python
import jax
import jax.numpy as jnp
import numpy as np
from jax import lax
from jax.experimental import pallas as pl
from jax.sharding import Mesh
from jax.sharding import PartitionSpec as P

HEAD_DIM = 64
SPAN = 128
LEFT = 1024
KERNEL = 9
TM = ("x", "y", "core")


def passed_along(value, axis, steps):
    count = lax.axis_size(axis)
    first, last = (max(0, -steps), min(count, count - steps))
    return lax.ppermute(value, axis, [(source, source + steps) for source in range(first, last)])


def with_halo(cells, axis, width):
    count = lax.axis_size(axis)
    ends = count - 1
    head = lax.slice_in_dim(cells, 0, width, axis=0)
    tail = lax.slice_in_dim(cells, cells.shape[0] - width, cells.shape[0], axis=0)
    return jnp.concatenate(
        [
            lax.ppermute(tail, axis, [(i, (i + 1) % count) for i in range(ends)]),
            cells,
            lax.ppermute(head, axis, [((i + 1) % count, i) for i in range(ends)]),
        ],
        axis=0,
    )


def layer_norm(values, gain_vec):
    wide = values.astype(jnp.float32)
    center = wide - jnp.mean(wide, axis=-1, keepdims=True)
    spread = jnp.mean(center * center, axis=-1, keepdims=True)
    return center * lax.rsqrt(spread + 1e-05) * gain_vec


def contract_with(left, rows_piece):
    return jnp.dot(left, rows_piece, preferred_element_type=jnp.float32)


def attend_kernel(q_ref, k_ref, v_ref, m_ref, o_ref):
    width = q_ref.shape[1]
    heads = width // HEAD_DIM
    allowed = m_ref[...] > 0.5
    lane = lax.broadcasted_iota(jnp.int32, (1, width), 1)
    result = jnp.zeros(o_ref.shape, jnp.float32)
    for head in range(heads):
        inside = (lane >= head * HEAD_DIM) & (lane < (head + 1) * HEAD_DIM)
        query = jnp.where(inside, q_ref[...], jnp.zeros_like(q_ref[...]))
        scores = lax.dot_general(
            query, k_ref[...], (((1,), (1,)), ((), ())), preferred_element_type=jnp.float32
        ) * (1.0 / jnp.sqrt(jnp.float32(HEAD_DIM)))
        raised = jnp.where(allowed, jnp.exp(scores), 0.0)
        probs = (raised / jnp.sum(raised, axis=-1, keepdims=True)).astype(jnp.bfloat16)
        mixed = jnp.dot(probs, v_ref[...], preferred_element_type=jnp.float32)
        result = jnp.where(inside, mixed, result)
    o_ref[...] = result.astype(o_ref.dtype)

def attend(queries, key_value, allowed):
    rows, width = queries.shape
    keys = key_value.shape[0]
    tile = 128
    steps = width // tile
    return pl.pallas_call(
        attend_kernel,
        out_shape=jax.ShapeDtypeStruct((rows, width), jnp.bfloat16),
        grid=(steps,),
        in_specs=[
            pl.BlockSpec((rows, tile), lambda i: (0, i)),
            pl.BlockSpec((keys, tile), lambda i: (0, i)),
            pl.BlockSpec((keys, tile), lambda i: (0, i + steps)),
            pl.BlockSpec((rows, keys), lambda i: (0, 0)),
        ],
        out_specs=pl.BlockSpec((rows, tile), lambda i: (0, i)),
        cost_estimate=pl.CostEstimate(
            flops=4 * rows * keys * width * tile // HEAD_DIM,
            transcendentals=rows * keys * width // HEAD_DIM,
            bytes_accessed=2 * (2 * rows * width + 2 * keys * width) + 4 * rows * keys,
        ),
    )(queries, key_value, key_value, allowed.astype(jnp.float32))


def on_device(
    frames, lengths, ln_attn_gain, w_qkv, w_out, ln_conv_gain, w_pw1, dw_kernel, bn_gain, bn_bias
):
    stream = frames[0]
    frame_count, model_width = stream.shape
    head_count = model_width // HEAD_DIM
    length = lax.dynamic_index_in_dim(lengths, lax.axis_index("call"), 0, keepdims=False)
    first_row = lax.axis_index(TM) * frame_count
    query_pos = first_row + jnp.arange(frame_count, dtype=jnp.int32)
    frame_valid = query_pos < length
    qkv_cols = w_qkv.shape[1]
    out_cols = w_out.shape[1]
    weights = lax.all_gather(
        jnp.concatenate([w_qkv, w_out, w_pw1], axis=1), TM, axis=0, tiled=True
    )
    prior_blocks = LEFT // frame_count
    blocks = []
    current = stream
    for hop_index in range(prior_blocks):
        current = passed_along(current, TM, 1)
        blocks.append(current)
    context_frames = jnp.concatenate(blocks[::-1] + [stream], axis=0)
    key_count = context_frames.shape[0]
    normed_all = layer_norm(context_frames, ln_attn_gain).astype(jnp.bfloat16)
    normed = normed_all[key_count - frame_count :]
    queries = contract_with(normed, weights[:, :model_width]).astype(jnp.bfloat16)
    key_value = contract_with(normed_all, weights[:, model_width:qkv_cols]).astype(jnp.bfloat16)
    key_pos = first_row - prior_blocks * frame_count + jnp.arange(key_count, dtype=jnp.int32)
    span_first = query_pos // SPAN * SPAN
    allowed = (key_pos[None, :] >= 0) & (key_pos[None, :] >= span_first[:, None] - LEFT)
    allowed = allowed & (key_pos[None, :] < span_first[:, None] + SPAN)
    allowed = allowed & ((key_pos[None, :] < length) | (key_pos[None, :] == query_pos[:, None]))
    context = attend(queries, key_value, allowed)
    projected = contract_with(context, weights[:, qkv_cols : qkv_cols + out_cols])
    attended = jnp.where(frame_valid[:, None], stream.astype(jnp.float32) + projected, 0.0).astype(
        jnp.bfloat16
    )
    conv_in = layer_norm(attended, ln_conv_gain).astype(jnp.bfloat16)
    expanded = contract_with(conv_in, weights[:, qkv_cols + out_cols :])
    gated = expanded[:, :model_width] * jax.nn.sigmoid(expanded[:, model_width:])
    gated = jnp.where(frame_valid[:, None], gated, 0.0).astype(jnp.bfloat16)
    padded = with_halo(gated, TM, KERNEL // 2)
    depthwise = jnp.zeros((frame_count, model_width), jnp.float32)
    for tap_index in range(KERNEL):
        depthwise = (
            depthwise
            + padded[tap_index : tap_index + frame_count].astype(jnp.float32) * dw_kernel[tap_index]
        )
    masked = jnp.where(frame_valid[:, None], depthwise, 0.0)
    moments = (jnp.sum(masked, axis=0), jnp.sum(masked * depthwise, axis=0))
    for axis in ("core", "y", "x", "call"):
        moments = lax.psum(moments, axis)
    first_moment, second_moment = moments
    count_all = jnp.sum(lengths).astype(jnp.float32)
    average = first_moment / count_all
    second = second_moment / count_all
    normal_act = (depthwise - average) * lax.rsqrt(
        second - average * average + 1e-05
    ) * bn_gain + bn_bias
    activated = normal_act * jax.nn.sigmoid(normal_act)
    conv_act = jnp.where(frame_valid[:, None], activated, 0.0).astype(jnp.bfloat16)
    return (attended[None], conv_act[None])


def physical_mesh(mesh):
    devices = mesh.devices
    calls, tms = devices.shape
    first = devices[0]
    xs = len({d.coords[0] for d in first})
    ys = len({d.coords[1] for d in first})
    cores = tms // (xs * ys)
    grid = np.array(
        [[(d.coords[0], d.coords[1], d.core_on_chip) for d in row] for row in devices]
    )
    expect = np.stack(
        np.meshgrid(np.arange(xs), np.arange(ys), np.arange(cores), indexing="ij"), -1
    ).reshape(-1, 3)
    grid = grid - grid[:, :1]
    assert (grid == expect[None]).all()
    return Mesh(devices.reshape(calls, xs, ys, cores), ("call",) + TM)


def solution(mesh):
    mesh4 = physical_mesh(mesh)
    rows = P(TM, None)
    stream = P("call", TM, None)
    return jax.shard_map(
        on_device,
        mesh=mesh4,
        in_specs=(stream, P(), P(), rows, rows, P(), rows, P(), P(), P()),
        out_specs=(stream, stream),
        check_vma=False,
    )
```

```python
import jax
import jax.numpy as jnp
import numpy as np
from jax import lax
from jax.experimental import pallas as pl
from jax.sharding import Mesh
from jax.sharding import PartitionSpec as P

HEAD_DIM = 64
SPAN = 128
LEFT = 1024
KERNEL = 9
TM = ("x", "y", "core")


def passed_along(value, axis, steps):
    count = lax.axis_size(axis)
    first, last = (max(0, -steps), min(count, count - steps))
    return lax.ppermute(value, axis, [(source, source + steps) for source in range(first, last)])


def with_halo(cells, axis, width):
    count = lax.axis_size(axis)
    ends = count - 1
    head = lax.slice_in_dim(cells, 0, width, axis=0)
    tail = lax.slice_in_dim(cells, cells.shape[0] - width, cells.shape[0], axis=0)
    return jnp.concatenate(
        [
            lax.ppermute(tail, axis, [(i, (i + 1) % count) for i in range(ends)]),
            cells,
            lax.ppermute(head, axis, [((i + 1) % count, i) for i in range(ends)]),
        ],
        axis=0,
    )


def layer_norm(values, gain_vec):
    wide = values.astype(jnp.float32)
    center = wide - jnp.mean(wide, axis=-1, keepdims=True)
    spread = jnp.mean(center * center, axis=-1, keepdims=True)
    return center * lax.rsqrt(spread + 1e-05) * gain_vec


def contract_with(left, rows_piece):
    return jnp.dot(left, rows_piece, preferred_element_type=jnp.float32)


def attend_kernel(q_ref, k_ref, v_ref, m_ref, o_ref):
    width = q_ref.shape[1]
    heads = width // HEAD_DIM
    allowed = m_ref[...] > 0.5
    lane = lax.broadcasted_iota(jnp.int32, (1, width), 1)
    result = jnp.zeros(o_ref.shape, jnp.float32)
    for head in range(heads):
        inside = (lane >= head * HEAD_DIM) & (lane < (head + 1) * HEAD_DIM)
        query = jnp.where(inside, q_ref[...], jnp.zeros_like(q_ref[...]))
        scores = lax.dot_general(
            query, k_ref[...], (((1,), (1,)), ((), ())), preferred_element_type=jnp.float32
        ) * (1.0 / jnp.sqrt(jnp.float32(HEAD_DIM)))
        raised = jnp.where(allowed, jnp.exp(scores), 0.0)
        total = jnp.sum(raised, axis=-1, keepdims=True)
        mixed = jnp.dot(raised.astype(jnp.bfloat16), v_ref[...], preferred_element_type=jnp.float32)
        result = jnp.where(inside, mixed / total, result)
    o_ref[...] = result.astype(o_ref.dtype)

def attend(queries, key_value, allowed):
    rows, width = queries.shape
    keys = key_value.shape[0]
    tile = 128
    steps = width // tile
    return pl.pallas_call(
        attend_kernel,
        out_shape=jax.ShapeDtypeStruct((rows, width), jnp.bfloat16),
        grid=(steps,),
        in_specs=[
            pl.BlockSpec((rows, tile), lambda i: (0, i)),
            pl.BlockSpec((keys, tile), lambda i: (0, i)),
            pl.BlockSpec((keys, tile), lambda i: (0, i + steps)),
            pl.BlockSpec((rows, keys), lambda i: (0, 0)),
        ],
        out_specs=pl.BlockSpec((rows, tile), lambda i: (0, i)),
        cost_estimate=pl.CostEstimate(
            flops=4 * rows * keys * width * tile // HEAD_DIM,
            transcendentals=rows * keys * width // HEAD_DIM,
            bytes_accessed=2 * (2 * rows * width + 2 * keys * width) + 4 * rows * keys,
        ),
    )(queries, key_value, key_value, allowed.astype(jnp.float32))


def on_device(
    frames, lengths, ln_attn_gain, w_qkv, w_out, ln_conv_gain, w_pw1, dw_kernel, bn_gain, bn_bias
):
    stream = frames[0]
    frame_count, model_width = stream.shape
    head_count = model_width // HEAD_DIM
    length = lax.dynamic_index_in_dim(lengths, lax.axis_index("call"), 0, keepdims=False)
    first_row = lax.axis_index(TM) * frame_count
    query_pos = first_row + jnp.arange(frame_count, dtype=jnp.int32)
    frame_valid = query_pos < length
    qkv_cols = w_qkv.shape[1]
    out_cols = w_out.shape[1]
    weights = lax.all_gather(
        jnp.concatenate([w_qkv, w_out, w_pw1], axis=1), TM, axis=0, tiled=True
    )
    prior_blocks = LEFT // frame_count
    blocks = []
    current = stream
    for hop_index in range(prior_blocks):
        current = passed_along(current, TM, 1)
        blocks.append(current)
    context_frames = jnp.concatenate(blocks[::-1] + [stream], axis=0)
    key_count = context_frames.shape[0]
    normed_all = layer_norm(context_frames, ln_attn_gain).astype(jnp.bfloat16)
    normed = normed_all[key_count - frame_count :]
    queries = contract_with(normed, weights[:, :model_width]).astype(jnp.bfloat16)
    key_value = contract_with(normed_all, weights[:, model_width:qkv_cols]).astype(jnp.bfloat16)
    key_pos = first_row - prior_blocks * frame_count + jnp.arange(key_count, dtype=jnp.int32)
    span_first = query_pos // SPAN * SPAN
    allowed = (key_pos[None, :] >= 0) & (key_pos[None, :] >= span_first[:, None] - LEFT)
    allowed = allowed & (key_pos[None, :] < span_first[:, None] + SPAN)
    allowed = allowed & ((key_pos[None, :] < length) | (key_pos[None, :] == query_pos[:, None]))
    context = attend(queries, key_value, allowed)
    projected = contract_with(context, weights[:, qkv_cols : qkv_cols + out_cols])
    attended = jnp.where(frame_valid[:, None], stream.astype(jnp.float32) + projected, 0.0).astype(
        jnp.bfloat16
    )
    conv_in = layer_norm(attended, ln_conv_gain).astype(jnp.bfloat16)
    expanded = contract_with(conv_in, weights[:, qkv_cols + out_cols :])
    gated = expanded[:, :model_width] * jax.nn.sigmoid(expanded[:, model_width:])
    gated = jnp.where(frame_valid[:, None], gated, 0.0).astype(jnp.bfloat16)
    padded = with_halo(gated, TM, KERNEL // 2)
    depthwise = jnp.zeros((frame_count, model_width), jnp.float32)
    for tap_index in range(KERNEL):
        depthwise = (
            depthwise
            + padded[tap_index : tap_index + frame_count].astype(jnp.float32) * dw_kernel[tap_index]
        )
    masked = jnp.where(frame_valid[:, None], depthwise, 0.0)
    moments = (jnp.sum(masked, axis=0), jnp.sum(masked * depthwise, axis=0))
    for axis in ("core", "y", "x", "call"):
        moments = lax.psum(moments, axis)
    first_moment, second_moment = moments
    count_all = jnp.sum(lengths).astype(jnp.float32)
    average = first_moment / count_all
    second = second_moment / count_all
    normal_act = (depthwise - average) * lax.rsqrt(
        second - average * average + 1e-05
    ) * bn_gain + bn_bias
    activated = normal_act * jax.nn.sigmoid(normal_act)
    conv_act = jnp.where(frame_valid[:, None], activated, 0.0).astype(jnp.bfloat16)
    return (attended[None], conv_act[None])


def physical_mesh(mesh):
    devices = mesh.devices
    calls, tms = devices.shape
    first = devices[0]
    xs = len({d.coords[0] for d in first})
    ys = len({d.coords[1] for d in first})
    cores = tms // (xs * ys)
    grid = np.array(
        [[(d.coords[0], d.coords[1], d.core_on_chip) for d in row] for row in devices]
    )
    expect = np.stack(
        np.meshgrid(np.arange(xs), np.arange(ys), np.arange(cores), indexing="ij"), -1
    ).reshape(-1, 3)
    grid = grid - grid[:, :1]
    assert (grid == expect[None]).all()
    return Mesh(devices.reshape(calls, xs, ys, cores), ("call",) + TM)


def solution(mesh):
    mesh4 = physical_mesh(mesh)
    rows = P(TM, None)
    stream = P("call", TM, None)
    return jax.shard_map(
        on_device,
        mesh=mesh4,
        in_specs=(stream, P(), P(), rows, rows, P(), rows, P(), P(), P()),
        out_specs=(stream, stream),
        check_vma=False,
    )
```

```python
import jax
import jax.numpy as jnp
import numpy as np
from jax import lax
from jax.experimental import pallas as pl
from jax.sharding import Mesh
from jax.sharding import PartitionSpec as P

HEAD_DIM = 64
SPAN = 128
LEFT = 1024
KERNEL = 9
TM = ("x", "y", "core")


def passed_along(value, axis, steps):
    count = lax.axis_size(axis)
    first, last = (max(0, -steps), min(count, count - steps))
    return lax.ppermute(value, axis, [(source, source + steps) for source in range(first, last)])


def with_halo(cells, axis, width):
    count = lax.axis_size(axis)
    ends = count - 1
    head = lax.slice_in_dim(cells, 0, width, axis=0)
    tail = lax.slice_in_dim(cells, cells.shape[0] - width, cells.shape[0], axis=0)
    return jnp.concatenate(
        [
            lax.ppermute(tail, axis, [(i, (i + 1) % count) for i in range(ends)]),
            cells,
            lax.ppermute(head, axis, [((i + 1) % count, i) for i in range(ends)]),
        ],
        axis=0,
    )


def layer_norm(values, gain_vec):
    wide = values.astype(jnp.float32)
    center = wide - jnp.mean(wide, axis=-1, keepdims=True)
    spread = jnp.mean(center * center, axis=-1, keepdims=True)
    return center * lax.rsqrt(spread + 1e-05) * gain_vec


def contract_with(left, rows_piece):
    return jnp.dot(left, rows_piece, preferred_element_type=jnp.float32)


def attend_kernel(q_ref, k_ref, v_ref, m_ref, o_ref):
    width = q_ref.shape[1]
    heads = width // HEAD_DIM
    allowed = m_ref[...] > 0.5
    lane = lax.broadcasted_iota(jnp.int32, (1, width), 1)
    result = jnp.zeros(o_ref.shape, jnp.float32)
    for head in range(heads):
        inside = (lane >= head * HEAD_DIM) & (lane < (head + 1) * HEAD_DIM)
        query = jnp.where(inside, q_ref[...], jnp.zeros_like(q_ref[...]))
        scores = lax.dot_general(
            query, k_ref[...], (((1,), (1,)), ((), ())), preferred_element_type=jnp.float32
        ) * (1.0 / jnp.sqrt(jnp.float32(HEAD_DIM)))
        raised = jnp.where(allowed, jnp.exp(scores), 0.0)
        probs = (raised / jnp.sum(raised, axis=-1, keepdims=True)).astype(jnp.bfloat16)
        mixed = jnp.dot(probs, v_ref[...], preferred_element_type=jnp.float32)
        result = jnp.where(inside, mixed, result)
    o_ref[...] = result.astype(o_ref.dtype)

def attend(queries, key_value, allowed):
    rows, width = queries.shape
    keys = key_value.shape[0]
    tile = 4 * HEAD_DIM
    steps = width // tile
    return pl.pallas_call(
        attend_kernel,
        out_shape=jax.ShapeDtypeStruct((rows, width), jnp.bfloat16),
        grid=(steps,),
        in_specs=[
            pl.BlockSpec((rows, tile), lambda i: (0, i)),
            pl.BlockSpec((keys, tile), lambda i: (0, i)),
            pl.BlockSpec((keys, tile), lambda i: (0, i + steps)),
            pl.BlockSpec((rows, keys), lambda i: (0, 0)),
        ],
        out_specs=pl.BlockSpec((rows, tile), lambda i: (0, i)),
        cost_estimate=pl.CostEstimate(
            flops=4 * rows * keys * width * tile // HEAD_DIM,
            transcendentals=rows * keys * width // HEAD_DIM,
            bytes_accessed=2 * (2 * rows * width + 2 * keys * width) + 4 * rows * keys,
        ),
    )(queries, key_value, key_value, allowed.astype(jnp.float32))


def on_device(
    frames, lengths, ln_attn_gain, w_qkv, w_out, ln_conv_gain, w_pw1, dw_kernel, bn_gain, bn_bias
):
    stream = frames[0]
    frame_count, model_width = stream.shape
    head_count = model_width // HEAD_DIM
    length = lax.dynamic_index_in_dim(lengths, lax.axis_index("call"), 0, keepdims=False)
    first_row = lax.axis_index(TM) * frame_count
    query_pos = first_row + jnp.arange(frame_count, dtype=jnp.int32)
    frame_valid = query_pos < length
    qkv_cols = w_qkv.shape[1]
    out_cols = w_out.shape[1]
    weights = lax.all_gather(
        jnp.concatenate([w_qkv, w_out, w_pw1], axis=1), TM, axis=0, tiled=True
    )
    prior_blocks = LEFT // frame_count
    blocks = []
    current = stream
    for hop_index in range(prior_blocks):
        current = passed_along(current, TM, 1)
        blocks.append(current)
    context_frames = jnp.concatenate(blocks[::-1] + [stream], axis=0)
    key_count = context_frames.shape[0]
    normed_all = layer_norm(context_frames, ln_attn_gain).astype(jnp.bfloat16)
    normed = normed_all[key_count - frame_count :]
    queries = contract_with(normed, weights[:, :model_width]).astype(jnp.bfloat16)
    key_value = contract_with(normed_all, weights[:, model_width:qkv_cols]).astype(jnp.bfloat16)
    key_pos = first_row - prior_blocks * frame_count + jnp.arange(key_count, dtype=jnp.int32)
    span_first = query_pos // SPAN * SPAN
    allowed = (key_pos[None, :] >= 0) & (key_pos[None, :] >= span_first[:, None] - LEFT)
    allowed = allowed & (key_pos[None, :] < span_first[:, None] + SPAN)
    allowed = allowed & ((key_pos[None, :] < length) | (key_pos[None, :] == query_pos[:, None]))
    context = attend(queries, key_value, allowed)
    projected = contract_with(context, weights[:, qkv_cols : qkv_cols + out_cols])
    attended = jnp.where(frame_valid[:, None], stream.astype(jnp.float32) + projected, 0.0).astype(
        jnp.bfloat16
    )
    conv_in = layer_norm(attended, ln_conv_gain).astype(jnp.bfloat16)
    expanded = contract_with(conv_in, weights[:, qkv_cols + out_cols :])
    gated = expanded[:, :model_width] * jax.nn.sigmoid(expanded[:, model_width:])
    gated = jnp.where(frame_valid[:, None], gated, 0.0).astype(jnp.bfloat16)
    padded = with_halo(gated, TM, KERNEL // 2)
    depthwise = jnp.zeros((frame_count, model_width), jnp.float32)
    for tap_index in range(KERNEL):
        depthwise = (
            depthwise
            + padded[tap_index : tap_index + frame_count].astype(jnp.float32) * dw_kernel[tap_index]
        )
    masked = jnp.where(frame_valid[:, None], depthwise, 0.0)
    moments = (jnp.sum(masked, axis=0), jnp.sum(masked * depthwise, axis=0))
    for axis in ("core", "y", "x", "call"):
        moments = lax.psum(moments, axis)
    first_moment, second_moment = moments
    count_all = jnp.sum(lengths).astype(jnp.float32)
    average = first_moment / count_all
    second = second_moment / count_all
    normal_act = (depthwise - average) * lax.rsqrt(
        second - average * average + 1e-05
    ) * bn_gain + bn_bias
    activated = normal_act * jax.nn.sigmoid(normal_act)
    conv_act = jnp.where(frame_valid[:, None], activated, 0.0).astype(jnp.bfloat16)
    return (attended[None], conv_act[None])


def physical_mesh(mesh):
    devices = mesh.devices
    calls, tms = devices.shape
    first = devices[0]
    xs = len({d.coords[0] for d in first})
    ys = len({d.coords[1] for d in first})
    cores = tms // (xs * ys)
    grid = np.array(
        [[(d.coords[0], d.coords[1], d.core_on_chip) for d in row] for row in devices]
    )
    expect = np.stack(
        np.meshgrid(np.arange(xs), np.arange(ys), np.arange(cores), indexing="ij"), -1
    ).reshape(-1, 3)
    grid = grid - grid[:, :1]
    assert (grid == expect[None]).all()
    return Mesh(devices.reshape(calls, xs, ys, cores), ("call",) + TM)


def solution(mesh):
    mesh4 = physical_mesh(mesh)
    rows = P(TM, None)
    stream = P("call", TM, None)
    return jax.shard_map(
        on_device,
        mesh=mesh4,
        in_specs=(stream, P(), P(), rows, rows, P(), rows, P(), P(), P()),
        out_specs=(stream, stream),
        check_vma=False,
    )
```

```python
import jax
import jax.numpy as jnp
import numpy as np
from jax import lax
from jax.experimental import pallas as pl
from jax.sharding import Mesh
from jax.sharding import PartitionSpec as P

HEAD_DIM = 64
SPAN = 128
LEFT = 1024
KERNEL = 9
TM = ("x", "y", "core")


def passed_along(value, axis, steps):
    count = lax.axis_size(axis)
    first, last = (max(0, -steps), min(count, count - steps))
    return lax.ppermute(value, axis, [(source, source + steps) for source in range(first, last)])


def with_halo(cells, axis, width):
    count = lax.axis_size(axis)
    ends = count - 1
    head = lax.slice_in_dim(cells, 0, width, axis=0)
    tail = lax.slice_in_dim(cells, cells.shape[0] - width, cells.shape[0], axis=0)
    return jnp.concatenate(
        [
            lax.ppermute(tail, axis, [(i, (i + 1) % count) for i in range(ends)]),
            cells,
            lax.ppermute(head, axis, [((i + 1) % count, i) for i in range(ends)]),
        ],
        axis=0,
    )


def layer_norm(values, gain_vec):
    wide = values.astype(jnp.float32)
    center = wide - jnp.mean(wide, axis=-1, keepdims=True)
    spread = jnp.mean(center * center, axis=-1, keepdims=True)
    return center * lax.rsqrt(spread + 1e-05) * gain_vec


def contract_with(left, rows_piece):
    return jnp.dot(left, rows_piece, preferred_element_type=jnp.float32)


def attend_kernel(q_ref, k_ref, v_ref, m_ref, w_ref, o_ref):
    step = pl.program_id(0)
    width = q_ref.shape[1]
    heads = width // HEAD_DIM
    allowed = m_ref[...] > 0.5
    lane = lax.broadcasted_iota(jnp.int32, (1, width), 1)
    result = jnp.zeros(q_ref.shape, jnp.float32)
    for head in range(heads):
        inside = (lane >= head * HEAD_DIM) & (lane < (head + 1) * HEAD_DIM)
        query = jnp.where(inside, q_ref[...], jnp.zeros_like(q_ref[...]))
        scores = lax.dot_general(
            query, k_ref[...], (((1,), (1,)), ((), ())), preferred_element_type=jnp.float32
        ) * (1.0 / jnp.sqrt(jnp.float32(HEAD_DIM)))
        raised = jnp.where(allowed, jnp.exp(scores), 0.0)
        probs = (raised / jnp.sum(raised, axis=-1, keepdims=True)).astype(jnp.bfloat16)
        mixed = jnp.dot(probs, v_ref[...], preferred_element_type=jnp.float32)
        result = jnp.where(inside, mixed, result)
    part = jnp.dot(result.astype(jnp.bfloat16), w_ref[...], preferred_element_type=jnp.float32)

    @pl.when(step == 0)
    def _():
        o_ref[...] = part

    @pl.when(step > 0)
    def _():
        o_ref[...] += part


def attend(queries, key_value, allowed, weights, out_first):
    rows, width = queries.shape
    keys = key_value.shape[0]
    tile = 128
    steps = width // tile
    out_block = out_first // width
    return pl.pallas_call(
        attend_kernel,
        out_shape=jax.ShapeDtypeStruct((rows, width), jnp.float32),
        grid=(steps,),
        in_specs=[
            pl.BlockSpec((rows, tile), lambda i: (0, i)),
            pl.BlockSpec((keys, tile), lambda i: (0, i)),
            pl.BlockSpec((keys, tile), lambda i: (0, i + steps)),
            pl.BlockSpec((rows, keys), lambda i: (0, 0)),
            pl.BlockSpec((tile, width), lambda i: (i, out_block)),
        ],
        out_specs=pl.BlockSpec((rows, width), lambda i: (0, 0)),
        cost_estimate=pl.CostEstimate(
            flops=4 * rows * keys * width * tile // HEAD_DIM + 2 * rows * width * width,
            transcendentals=rows * keys * width // HEAD_DIM,
            bytes_accessed=2 * (2 * rows * width + 2 * keys * width + width * width)
            + 4 * rows * keys,
        ),
    )(queries, key_value, key_value, allowed.astype(jnp.float32), weights)


def on_device(
    frames, lengths, ln_attn_gain, w_qkv, w_out, ln_conv_gain, w_pw1, dw_kernel, bn_gain, bn_bias
):
    stream = frames[0]
    frame_count, model_width = stream.shape
    head_count = model_width // HEAD_DIM
    length = lax.dynamic_index_in_dim(lengths, lax.axis_index("call"), 0, keepdims=False)
    first_row = lax.axis_index(TM) * frame_count
    query_pos = first_row + jnp.arange(frame_count, dtype=jnp.int32)
    frame_valid = query_pos < length
    qkv_cols = w_qkv.shape[1]
    out_cols = w_out.shape[1]
    weights = lax.all_gather(
        jnp.concatenate([w_qkv, w_out, w_pw1], axis=1), TM, axis=0, tiled=True
    )
    prior_blocks = LEFT // frame_count
    blocks = []
    current = stream
    for hop_index in range(prior_blocks):
        current = passed_along(current, TM, 1)
        blocks.append(current)
    context_frames = jnp.concatenate(blocks[::-1] + [stream], axis=0)
    key_count = context_frames.shape[0]
    normed_all = layer_norm(context_frames, ln_attn_gain).astype(jnp.bfloat16)
    normed = normed_all[key_count - frame_count :]
    queries = contract_with(normed, weights[:, :model_width]).astype(jnp.bfloat16)
    key_value = contract_with(normed_all, weights[:, model_width:qkv_cols]).astype(jnp.bfloat16)
    key_pos = first_row - prior_blocks * frame_count + jnp.arange(key_count, dtype=jnp.int32)
    span_first = query_pos // SPAN * SPAN
    allowed = (key_pos[None, :] >= 0) & (key_pos[None, :] >= span_first[:, None] - LEFT)
    allowed = allowed & (key_pos[None, :] < span_first[:, None] + SPAN)
    allowed = allowed & ((key_pos[None, :] < length) | (key_pos[None, :] == query_pos[:, None]))
    projected = attend(queries, key_value, allowed, weights, qkv_cols)
    attended = jnp.where(frame_valid[:, None], stream.astype(jnp.float32) + projected, 0.0).astype(
        jnp.bfloat16
    )
    conv_in = layer_norm(attended, ln_conv_gain).astype(jnp.bfloat16)
    expanded = contract_with(conv_in, weights[:, qkv_cols + out_cols :])
    gated = expanded[:, :model_width] * jax.nn.sigmoid(expanded[:, model_width:])
    gated = jnp.where(frame_valid[:, None], gated, 0.0).astype(jnp.bfloat16)
    padded = with_halo(gated, TM, KERNEL // 2)
    depthwise = jnp.zeros((frame_count, model_width), jnp.float32)
    for tap_index in range(KERNEL):
        depthwise = (
            depthwise
            + padded[tap_index : tap_index + frame_count].astype(jnp.float32) * dw_kernel[tap_index]
        )
    masked = jnp.where(frame_valid[:, None], depthwise, 0.0)
    moments = (jnp.sum(masked, axis=0), jnp.sum(masked * depthwise, axis=0))
    for axis in ("core", "y", "x", "call"):
        moments = lax.psum(moments, axis)
    first_moment, second_moment = moments
    count_all = jnp.sum(lengths).astype(jnp.float32)
    average = first_moment / count_all
    second = second_moment / count_all
    normal_act = (depthwise - average) * lax.rsqrt(
        second - average * average + 1e-05
    ) * bn_gain + bn_bias
    activated = normal_act * jax.nn.sigmoid(normal_act)
    conv_act = jnp.where(frame_valid[:, None], activated, 0.0).astype(jnp.bfloat16)
    return (attended[None], conv_act[None])


def physical_mesh(mesh):
    devices = mesh.devices
    calls, tms = devices.shape
    first = devices[0]
    xs = len({d.coords[0] for d in first})
    ys = len({d.coords[1] for d in first})
    cores = tms // (xs * ys)
    grid = np.array(
        [[(d.coords[0], d.coords[1], d.core_on_chip) for d in row] for row in devices]
    )
    expect = np.stack(
        np.meshgrid(np.arange(xs), np.arange(ys), np.arange(cores), indexing="ij"), -1
    ).reshape(-1, 3)
    grid = grid - grid[:, :1]
    assert (grid == expect[None]).all()
    return Mesh(devices.reshape(calls, xs, ys, cores), ("call",) + TM)


def solution(mesh):
    mesh4 = physical_mesh(mesh)
    rows = P(TM, None)
    stream = P("call", TM, None)
    return jax.shard_map(
        on_device,
        mesh=mesh4,
        in_specs=(stream, P(), P(), rows, rows, P(), rows, P(), P(), P()),
        out_specs=(stream, stream),
        check_vma=False,
    )
```

```python
import jax
import jax.numpy as jnp
import numpy as np
from jax import lax
from jax.experimental import pallas as pl
from jax.sharding import Mesh
from jax.sharding import PartitionSpec as P

HEAD_DIM = 64
SPAN = 128
LEFT = 1024
KERNEL = 9
TM = ("x", "y", "core")


def passed_along(value, axis, steps):
    count = lax.axis_size(axis)
    first, last = (max(0, -steps), min(count, count - steps))
    return lax.ppermute(value, axis, [(source, source + steps) for source in range(first, last)])


def with_halo(cells, axis, width):
    count = lax.axis_size(axis)
    ends = count - 1
    head = lax.slice_in_dim(cells, 0, width, axis=0)
    tail = lax.slice_in_dim(cells, cells.shape[0] - width, cells.shape[0], axis=0)
    return jnp.concatenate(
        [
            lax.ppermute(tail, axis, [(i, (i + 1) % count) for i in range(ends)]),
            cells,
            lax.ppermute(head, axis, [((i + 1) % count, i) for i in range(ends)]),
        ],
        axis=0,
    )


def layer_norm(values, gain_vec):
    wide = values.astype(jnp.float32)
    center = wide - jnp.mean(wide, axis=-1, keepdims=True)
    spread = jnp.mean(center * center, axis=-1, keepdims=True)
    return center * lax.rsqrt(spread + 1e-05) * gain_vec


def contract_with(left, rows_piece):
    return jnp.dot(left, rows_piece, preferred_element_type=jnp.float32)


def attend_kernel(q_ref, k_ref, v_ref, m_ref, o_ref):
    width = q_ref.shape[1]
    heads = width // HEAD_DIM
    allowed = m_ref[...] > 0.5
    lane = lax.broadcasted_iota(jnp.int32, (1, width), 1)
    result = jnp.zeros(o_ref.shape, jnp.float32)
    for head in range(heads):
        inside = (lane >= head * HEAD_DIM) & (lane < (head + 1) * HEAD_DIM)
        query = jnp.where(inside, q_ref[...], jnp.zeros_like(q_ref[...]))
        scores = lax.dot_general(
            query, k_ref[...], (((1,), (1,)), ((), ())), preferred_element_type=jnp.float32
        ) * (1.0 / jnp.sqrt(jnp.float32(HEAD_DIM)))
        raised = jnp.where(allowed, jnp.exp(scores), 0.0)
        probs = (raised / jnp.sum(raised, axis=-1, keepdims=True)).astype(jnp.bfloat16)
        mixed = jnp.dot(probs, v_ref[...], preferred_element_type=jnp.float32)
        result = jnp.where(inside, mixed, result)
    o_ref[...] = result.astype(o_ref.dtype)

def attend(queries, key_value, allowed):
    rows, width = queries.shape
    keys = key_value.shape[0]
    tile = 128
    steps = width // tile
    return pl.pallas_call(
        attend_kernel,
        out_shape=jax.ShapeDtypeStruct((rows, width), jnp.bfloat16),
        grid=(steps,),
        in_specs=[
            pl.BlockSpec((rows, tile), lambda i: (0, i)),
            pl.BlockSpec((keys, tile), lambda i: (0, i)),
            pl.BlockSpec((keys, tile), lambda i: (0, i + steps)),
            pl.BlockSpec((rows, keys), lambda i: (0, 0)),
        ],
        out_specs=pl.BlockSpec((rows, tile), lambda i: (0, i)),
        cost_estimate=pl.CostEstimate(
            flops=4 * rows * keys * width * tile // HEAD_DIM,
            transcendentals=rows * keys * width // HEAD_DIM,
            bytes_accessed=2 * (2 * rows * width + 2 * keys * width) + 4 * rows * keys,
        ),
    )(queries, key_value, key_value, allowed.astype(jnp.float32))


def on_device(
    frames, lengths, ln_attn_gain, w_qkv, w_out, ln_conv_gain, w_pw1, dw_kernel, bn_gain, bn_bias
):
    stream = frames[0]
    frame_count, model_width = stream.shape
    head_count = model_width // HEAD_DIM
    length = lax.dynamic_index_in_dim(lengths, lax.axis_index("call"), 0, keepdims=False)
    first_row = lax.axis_index(TM) * frame_count
    query_pos = first_row + jnp.arange(frame_count, dtype=jnp.int32)
    frame_valid = query_pos < length
    qkv_cols = w_qkv.shape[1]
    out_cols = w_out.shape[1]
    weights = lax.all_gather(
        jnp.concatenate([w_qkv, w_out, w_pw1], axis=1), TM, axis=0, tiled=True
    )
    prior_blocks = LEFT // frame_count
    blocks = []
    current = stream
    for hop_index in range(prior_blocks):
        current = passed_along(current, TM, 1)
        blocks.append(current)
    context_frames = jnp.concatenate(blocks[::-1] + [stream], axis=0)
    key_count = context_frames.shape[0]
    normed_all = layer_norm(context_frames, ln_attn_gain).astype(jnp.bfloat16)
    normed = normed_all[key_count - frame_count :]
    queries = contract_with(normed, weights[:, :model_width]).astype(jnp.bfloat16)
    key_value = contract_with(normed_all, weights[:, model_width:qkv_cols]).astype(jnp.bfloat16)
    key_pos = first_row - prior_blocks * frame_count + jnp.arange(key_count, dtype=jnp.int32)
    span_first = query_pos // SPAN * SPAN
    allowed = (key_pos[None, :] >= 0) & (key_pos[None, :] >= span_first[:, None] - LEFT)
    allowed = allowed & (key_pos[None, :] < span_first[:, None] + SPAN)
    allowed = allowed & ((key_pos[None, :] < length) | (key_pos[None, :] == query_pos[:, None]))
    context = attend(queries, key_value, allowed)
    projected = contract_with(context, weights[:, qkv_cols : qkv_cols + out_cols])
    attended = jnp.where(frame_valid[:, None], stream.astype(jnp.float32) + projected, 0.0).astype(
        jnp.bfloat16
    )
    conv_in = layer_norm(attended, ln_conv_gain).astype(jnp.bfloat16)
    expanded = contract_with(conv_in, weights[:, qkv_cols + out_cols :])
    gated = expanded[:, :model_width] * jax.nn.sigmoid(expanded[:, model_width:])
    gated = jnp.where(frame_valid[:, None], gated, 0.0).astype(jnp.bfloat16)
    padded = with_halo(gated, TM, KERNEL // 2)
    depthwise = jnp.zeros((frame_count, model_width), jnp.float32)
    for tap_index in range(KERNEL):
        depthwise = (
            depthwise
            + padded[tap_index : tap_index + frame_count].astype(jnp.float32) * dw_kernel[tap_index]
        )
    masked = jnp.where(frame_valid[:, None], depthwise, 0.0)
    moments = jnp.concatenate([jnp.sum(masked, axis=0), jnp.sum(masked * depthwise, axis=0)])
    for axis in ("core", "y", "x", "call"):
        moments = lax.psum(moments, axis)
    first_moment, second_moment = moments[:model_width], moments[model_width:]
    count_all = jnp.sum(lengths).astype(jnp.float32)
    average = first_moment / count_all
    second = second_moment / count_all
    normal_act = (depthwise - average) * lax.rsqrt(
        second - average * average + 1e-05
    ) * bn_gain + bn_bias
    activated = normal_act * jax.nn.sigmoid(normal_act)
    conv_act = jnp.where(frame_valid[:, None], activated, 0.0).astype(jnp.bfloat16)
    return (attended[None], conv_act[None])


def physical_mesh(mesh):
    devices = mesh.devices
    calls, tms = devices.shape
    first = devices[0]
    xs = len({d.coords[0] for d in first})
    ys = len({d.coords[1] for d in first})
    cores = tms // (xs * ys)
    grid = np.array(
        [[(d.coords[0], d.coords[1], d.core_on_chip) for d in row] for row in devices]
    )
    expect = np.stack(
        np.meshgrid(np.arange(xs), np.arange(ys), np.arange(cores), indexing="ij"), -1
    ).reshape(-1, 3)
    grid = grid - grid[:, :1]
    assert (grid == expect[None]).all()
    return Mesh(devices.reshape(calls, xs, ys, cores), ("call",) + TM)


def solution(mesh):
    mesh4 = physical_mesh(mesh)
    rows = P(TM, None)
    stream = P("call", TM, None)
    return jax.shard_map(
        on_device,
        mesh=mesh4,
        in_specs=(stream, P(), P(), rows, rows, P(), rows, P(), P(), P()),
        out_specs=(stream, stream),
        check_vma=False,
    )
```

```python
import jax
import jax.numpy as jnp
import numpy as np
from jax import lax
from jax.experimental import pallas as pl
from jax.sharding import Mesh
from jax.sharding import PartitionSpec as P

HEAD_DIM = 64
SPAN = 128
LEFT = 1024
KERNEL = 9
TM = ("x", "y", "core")


def passed_along(value, axis, steps):
    count = lax.axis_size(axis)
    first, last = (max(0, -steps), min(count, count - steps))
    return lax.ppermute(value, axis, [(source, source + steps) for source in range(first, last)])


def with_halo(cells, axis, width):
    count = lax.axis_size(axis)
    ends = count - 1
    head = lax.slice_in_dim(cells, 0, width, axis=0)
    tail = lax.slice_in_dim(cells, cells.shape[0] - width, cells.shape[0], axis=0)
    return jnp.concatenate(
        [
            lax.ppermute(tail, axis, [(i, (i + 1) % count) for i in range(ends)]),
            cells,
            lax.ppermute(head, axis, [((i + 1) % count, i) for i in range(ends)]),
        ],
        axis=0,
    )


def layer_norm(values, gain_vec):
    wide = values.astype(jnp.float32)
    center = wide - jnp.mean(wide, axis=-1, keepdims=True)
    spread = jnp.mean(center * center, axis=-1, keepdims=True)
    return center * lax.rsqrt(spread + 1e-05) * gain_vec


def contract_with(left, rows_piece):
    return jnp.dot(left, rows_piece, preferred_element_type=jnp.float32)


def attend_kernel(q_ref, k_ref, v_ref, m_ref, o_ref):
    width = q_ref.shape[1]
    heads = width // HEAD_DIM
    allowed = m_ref[...] > 0.5
    lane = lax.broadcasted_iota(jnp.int32, (1, width), 1)
    result = jnp.zeros(o_ref.shape, jnp.float32)
    for head in range(heads):
        inside = (lane >= head * HEAD_DIM) & (lane < (head + 1) * HEAD_DIM)
        query = jnp.where(inside, q_ref[...], jnp.zeros_like(q_ref[...]))
        scores = lax.dot_general(
            query, k_ref[...], (((1,), (1,)), ((), ())), preferred_element_type=jnp.float32
        ) * (1.0 / jnp.sqrt(jnp.float32(HEAD_DIM)))
        raised = jnp.where(allowed, jnp.exp(scores), 0.0)
        probs = (raised / jnp.sum(raised, axis=-1, keepdims=True)).astype(jnp.bfloat16)
        mixed = jnp.dot(probs, v_ref[...], preferred_element_type=jnp.float32)
        result = jnp.where(inside, mixed, result)
    o_ref[...] = result.astype(o_ref.dtype)

def attend(queries, key_value, allowed):
    rows, width = queries.shape
    keys = key_value.shape[0]
    tile = 128
    steps = width // tile
    return pl.pallas_call(
        attend_kernel,
        out_shape=jax.ShapeDtypeStruct((rows, width), jnp.bfloat16),
        grid=(steps,),
        in_specs=[
            pl.BlockSpec((rows, tile), lambda i: (0, i)),
            pl.BlockSpec((keys, tile), lambda i: (0, i)),
            pl.BlockSpec((keys, tile), lambda i: (0, i + steps)),
            pl.BlockSpec((rows, keys), lambda i: (0, 0)),
        ],
        out_specs=pl.BlockSpec((rows, tile), lambda i: (0, i)),
        cost_estimate=pl.CostEstimate(
            flops=4 * rows * keys * width * tile // HEAD_DIM,
            transcendentals=rows * keys * width // HEAD_DIM,
            bytes_accessed=2 * (2 * rows * width + 2 * keys * width) + 4 * rows * keys,
        ),
    )(queries, key_value, key_value, allowed.astype(jnp.float32))


def on_device(
    frames, lengths, ln_attn_gain, w_qkv, w_out, ln_conv_gain, w_pw1, dw_kernel, bn_gain, bn_bias
):
    stream = frames[0]
    frame_count, model_width = stream.shape
    head_count = model_width // HEAD_DIM
    length = lax.dynamic_index_in_dim(lengths, lax.axis_index("call"), 0, keepdims=False)
    first_row = lax.axis_index(TM) * frame_count
    query_pos = first_row + jnp.arange(frame_count, dtype=jnp.int32)
    frame_valid = query_pos < length
    qkv_cols = w_qkv.shape[1]
    out_cols = w_out.shape[1]
    packed = jnp.zeros((w_qkv.shape[0], qkv_cols + out_cols + w_pw1.shape[1]), w_qkv.dtype)
    packed = lax.dynamic_update_slice(packed, w_qkv, (0, 0))
    packed = lax.dynamic_update_slice(packed, w_out, (0, qkv_cols))
    packed = lax.dynamic_update_slice(packed, w_pw1, (0, qkv_cols + out_cols))
    weights = lax.all_gather(packed, TM, axis=0, tiled=True)
    prior_blocks = LEFT // frame_count
    blocks = []
    current = stream
    for hop_index in range(prior_blocks):
        current = passed_along(current, TM, 1)
        blocks.append(current)
    context_frames = jnp.concatenate(blocks[::-1] + [stream], axis=0)
    key_count = context_frames.shape[0]
    normed_all = layer_norm(context_frames, ln_attn_gain).astype(jnp.bfloat16)
    normed = normed_all[key_count - frame_count :]
    queries = contract_with(normed, weights[:, :model_width]).astype(jnp.bfloat16)
    key_value = contract_with(normed_all, weights[:, model_width:qkv_cols]).astype(jnp.bfloat16)
    key_pos = first_row - prior_blocks * frame_count + jnp.arange(key_count, dtype=jnp.int32)
    span_first = query_pos // SPAN * SPAN
    allowed = (key_pos[None, :] >= 0) & (key_pos[None, :] >= span_first[:, None] - LEFT)
    allowed = allowed & (key_pos[None, :] < span_first[:, None] + SPAN)
    allowed = allowed & ((key_pos[None, :] < length) | (key_pos[None, :] == query_pos[:, None]))
    context = attend(queries, key_value, allowed)
    projected = contract_with(context, weights[:, qkv_cols : qkv_cols + out_cols])
    attended = jnp.where(frame_valid[:, None], stream.astype(jnp.float32) + projected, 0.0).astype(
        jnp.bfloat16
    )
    conv_in = layer_norm(attended, ln_conv_gain).astype(jnp.bfloat16)
    expanded = contract_with(conv_in, weights[:, qkv_cols + out_cols :])
    gated = expanded[:, :model_width] * jax.nn.sigmoid(expanded[:, model_width:])
    gated = jnp.where(frame_valid[:, None], gated, 0.0).astype(jnp.bfloat16)
    padded = with_halo(gated, TM, KERNEL // 2)
    depthwise = jnp.zeros((frame_count, model_width), jnp.float32)
    for tap_index in range(KERNEL):
        depthwise = (
            depthwise
            + padded[tap_index : tap_index + frame_count].astype(jnp.float32) * dw_kernel[tap_index]
        )
    masked = jnp.where(frame_valid[:, None], depthwise, 0.0)
    moments = jnp.concatenate([jnp.sum(masked, axis=0), jnp.sum(masked * depthwise, axis=0)])
    for axis in ("core", "y", "x", "call"):
        moments = lax.psum(moments, axis)
    first_moment, second_moment = moments[:model_width], moments[model_width:]
    count_all = jnp.sum(lengths).astype(jnp.float32)
    average = first_moment / count_all
    second = second_moment / count_all
    normal_act = (depthwise - average) * lax.rsqrt(
        second - average * average + 1e-05
    ) * bn_gain + bn_bias
    activated = normal_act * jax.nn.sigmoid(normal_act)
    conv_act = jnp.where(frame_valid[:, None], activated, 0.0).astype(jnp.bfloat16)
    return (attended[None], conv_act[None])


def physical_mesh(mesh):
    devices = mesh.devices
    calls, tms = devices.shape
    first = devices[0]
    xs = len({d.coords[0] for d in first})
    ys = len({d.coords[1] for d in first})
    cores = tms // (xs * ys)
    grid = np.array(
        [[(d.coords[0], d.coords[1], d.core_on_chip) for d in row] for row in devices]
    )
    expect = np.stack(
        np.meshgrid(np.arange(xs), np.arange(ys), np.arange(cores), indexing="ij"), -1
    ).reshape(-1, 3)
    grid = grid - grid[:, :1]
    assert (grid == expect[None]).all()
    return Mesh(devices.reshape(calls, xs, ys, cores), ("call",) + TM)


def solution(mesh):
    mesh4 = physical_mesh(mesh)
    rows = P(TM, None)
    stream = P("call", TM, None)
    return jax.shard_map(
        on_device,
        mesh=mesh4,
        in_specs=(stream, P(), P(), rows, rows, P(), rows, P(), P(), P()),
        out_specs=(stream, stream),
        check_vma=False,
    )
```

```python
import jax
import jax.numpy as jnp
import numpy as np
from jax import lax
from jax.experimental import pallas as pl
from jax.sharding import Mesh
from jax.sharding import PartitionSpec as P

HEAD_DIM = 64
SPAN = 128
LEFT = 1024
KERNEL = 9
TM = ("x", "y", "core")


def passed_along(value, axis, steps):
    count = lax.axis_size(axis)
    first, last = (max(0, -steps), min(count, count - steps))
    return lax.ppermute(value, axis, [(source, source + steps) for source in range(first, last)])


def with_halo(cells, axis, width):
    count = lax.axis_size(axis)
    ends = count - 1
    head = lax.slice_in_dim(cells, 0, width, axis=0)
    tail = lax.slice_in_dim(cells, cells.shape[0] - width, cells.shape[0], axis=0)
    return jnp.concatenate(
        [
            lax.ppermute(tail, axis, [(i, (i + 1) % count) for i in range(ends)]),
            cells,
            lax.ppermute(head, axis, [((i + 1) % count, i) for i in range(ends)]),
        ],
        axis=0,
    )


def layer_norm(values, gain_vec):
    wide = values.astype(jnp.float32)
    center = wide - jnp.mean(wide, axis=-1, keepdims=True)
    spread = jnp.mean(center * center, axis=-1, keepdims=True)
    return center * lax.rsqrt(spread + 1e-05) * gain_vec


def contract_with(left, rows_piece):
    return jnp.dot(left, rows_piece, preferred_element_type=jnp.float32)


def attend_kernel(x_ref, wq_ref, k_ref, v_ref, m_ref, o_ref):
    width = o_ref.shape[1]
    heads = width // HEAD_DIM
    allowed = m_ref[...] > 0.5
    lane = lax.broadcasted_iota(jnp.int32, (1, width), 1)
    queries = jnp.dot(x_ref[...], wq_ref[...], preferred_element_type=jnp.float32)
    queries = queries.astype(jnp.bfloat16)
    result = jnp.zeros(o_ref.shape, jnp.float32)
    for head in range(heads):
        inside = (lane >= head * HEAD_DIM) & (lane < (head + 1) * HEAD_DIM)
        query = jnp.where(inside, queries, jnp.zeros_like(queries))
        scores = lax.dot_general(
            query, k_ref[...], (((1,), (1,)), ((), ())), preferred_element_type=jnp.float32
        ) * (1.0 / jnp.sqrt(jnp.float32(HEAD_DIM)))
        raised = jnp.where(allowed, jnp.exp(scores), 0.0)
        probs = (raised / jnp.sum(raised, axis=-1, keepdims=True)).astype(jnp.bfloat16)
        mixed = jnp.dot(probs, v_ref[...], preferred_element_type=jnp.float32)
        result = jnp.where(inside, mixed, result)
    o_ref[...] = result.astype(o_ref.dtype)


def attend(normed, weights, key_value, allowed):
    rows, width = normed.shape
    keys = key_value.shape[0]
    tile = 128
    steps = width // tile
    return pl.pallas_call(
        attend_kernel,
        out_shape=jax.ShapeDtypeStruct((rows, width), jnp.bfloat16),
        grid=(steps,),
        in_specs=[
            pl.BlockSpec((rows, width), lambda i: (0, 0)),
            pl.BlockSpec((width, tile), lambda i: (0, i)),
            pl.BlockSpec((keys, tile), lambda i: (0, i)),
            pl.BlockSpec((keys, tile), lambda i: (0, i + steps)),
            pl.BlockSpec((rows, keys), lambda i: (0, 0)),
        ],
        out_specs=pl.BlockSpec((rows, tile), lambda i: (0, i)),
        cost_estimate=pl.CostEstimate(
            flops=4 * rows * keys * width * tile // HEAD_DIM + 2 * rows * width * width,
            transcendentals=rows * keys * width // HEAD_DIM,
            bytes_accessed=2 * (2 * rows * width + 2 * keys * width + width * width)
            + 4 * rows * keys,
        ),
    )(normed, weights, key_value, key_value, allowed.astype(jnp.float32))


def on_device(
    frames, lengths, ln_attn_gain, w_qkv, w_out, ln_conv_gain, w_pw1, dw_kernel, bn_gain, bn_bias
):
    stream = frames[0]
    frame_count, model_width = stream.shape
    head_count = model_width // HEAD_DIM
    length = lax.dynamic_index_in_dim(lengths, lax.axis_index("call"), 0, keepdims=False)
    first_row = lax.axis_index(TM) * frame_count
    query_pos = first_row + jnp.arange(frame_count, dtype=jnp.int32)
    frame_valid = query_pos < length
    qkv_cols = w_qkv.shape[1]
    out_cols = w_out.shape[1]
    weights = lax.all_gather(
        jnp.concatenate([w_qkv, w_out, w_pw1], axis=1), TM, axis=0, tiled=True
    )
    prior_blocks = LEFT // frame_count
    blocks = []
    current = stream
    for hop_index in range(prior_blocks):
        current = passed_along(current, TM, 1)
        blocks.append(current)
    context_frames = jnp.concatenate(blocks[::-1] + [stream], axis=0)
    key_count = context_frames.shape[0]
    normed_all = layer_norm(context_frames, ln_attn_gain).astype(jnp.bfloat16)
    normed = normed_all[key_count - frame_count :]
    key_value = contract_with(normed_all, weights[:, model_width:qkv_cols]).astype(jnp.bfloat16)
    key_pos = first_row - prior_blocks * frame_count + jnp.arange(key_count, dtype=jnp.int32)
    span_first = query_pos // SPAN * SPAN
    allowed = (key_pos[None, :] >= 0) & (key_pos[None, :] >= span_first[:, None] - LEFT)
    allowed = allowed & (key_pos[None, :] < span_first[:, None] + SPAN)
    allowed = allowed & ((key_pos[None, :] < length) | (key_pos[None, :] == query_pos[:, None]))
    context = attend(normed, weights, key_value, allowed)
    projected = contract_with(context, weights[:, qkv_cols : qkv_cols + out_cols])
    attended = jnp.where(frame_valid[:, None], stream.astype(jnp.float32) + projected, 0.0).astype(
        jnp.bfloat16
    )
    conv_in = layer_norm(attended, ln_conv_gain).astype(jnp.bfloat16)
    expanded = contract_with(conv_in, weights[:, qkv_cols + out_cols :])
    gated = expanded[:, :model_width] * jax.nn.sigmoid(expanded[:, model_width:])
    gated = jnp.where(frame_valid[:, None], gated, 0.0).astype(jnp.bfloat16)
    padded = with_halo(gated, TM, KERNEL // 2)
    depthwise = jnp.zeros((frame_count, model_width), jnp.float32)
    for tap_index in range(KERNEL):
        depthwise = (
            depthwise
            + padded[tap_index : tap_index + frame_count].astype(jnp.float32) * dw_kernel[tap_index]
        )
    masked = jnp.where(frame_valid[:, None], depthwise, 0.0)
    moments = (jnp.sum(masked, axis=0), jnp.sum(masked * depthwise, axis=0))
    for axis in ("core", "y", "x", "call"):
        moments = lax.psum(moments, axis)
    first_moment, second_moment = moments
    count_all = jnp.sum(lengths).astype(jnp.float32)
    average = first_moment / count_all
    second = second_moment / count_all
    normal_act = (depthwise - average) * lax.rsqrt(
        second - average * average + 1e-05
    ) * bn_gain + bn_bias
    activated = normal_act * jax.nn.sigmoid(normal_act)
    conv_act = jnp.where(frame_valid[:, None], activated, 0.0).astype(jnp.bfloat16)
    return (attended[None], conv_act[None])


def physical_mesh(mesh):
    devices = mesh.devices
    calls, tms = devices.shape
    first = devices[0]
    xs = len({d.coords[0] for d in first})
    ys = len({d.coords[1] for d in first})
    cores = tms // (xs * ys)
    grid = np.array(
        [[(d.coords[0], d.coords[1], d.core_on_chip) for d in row] for row in devices]
    )
    expect = np.stack(
        np.meshgrid(np.arange(xs), np.arange(ys), np.arange(cores), indexing="ij"), -1
    ).reshape(-1, 3)
    grid = grid - grid[:, :1]
    assert (grid == expect[None]).all()
    return Mesh(devices.reshape(calls, xs, ys, cores), ("call",) + TM)


def solution(mesh):
    mesh4 = physical_mesh(mesh)
    rows = P(TM, None)
    stream = P("call", TM, None)
    return jax.shard_map(
        on_device,
        mesh=mesh4,
        in_specs=(stream, P(), P(), rows, rows, P(), rows, P(), P(), P()),
        out_specs=(stream, stream),
        check_vma=False,
    )
```

```python
import jax
import jax.numpy as jnp
import numpy as np
from jax import lax
from jax.experimental import pallas as pl
from jax.sharding import Mesh
from jax.sharding import PartitionSpec as P

HEAD_DIM = 64
SPAN = 128
LEFT = 1024
KERNEL = 9
TM = ("x", "y", "core")


def passed_along(value, axis, steps):
    count = lax.axis_size(axis)
    first, last = (max(0, -steps), min(count, count - steps))
    return lax.ppermute(value, axis, [(source, source + steps) for source in range(first, last)])


def with_halo(cells, axis, width):
    count = lax.axis_size(axis)
    ends = count - 1
    head = lax.slice_in_dim(cells, 0, width, axis=0)
    tail = lax.slice_in_dim(cells, cells.shape[0] - width, cells.shape[0], axis=0)
    return jnp.concatenate(
        [
            lax.ppermute(tail, axis, [(i, (i + 1) % count) for i in range(ends)]),
            cells,
            lax.ppermute(head, axis, [((i + 1) % count, i) for i in range(ends)]),
        ],
        axis=0,
    )


def layer_norm(values, gain_vec):
    wide = values.astype(jnp.float32)
    center = wide - jnp.mean(wide, axis=-1, keepdims=True)
    spread = jnp.mean(center * center, axis=-1, keepdims=True)
    return center * lax.rsqrt(spread + 1e-05) * gain_vec


def contract_with(left, rows_piece):
    return jnp.dot(left, rows_piece, preferred_element_type=jnp.float32)


def attend_kernel(x_ref, wq_ref, wk_ref, wv_ref, m_ref, o_ref):
    rows, width = o_ref.shape
    heads = width // HEAD_DIM
    allowed = m_ref[...] > 0.5
    lane = lax.broadcasted_iota(jnp.int32, (1, width), 1)
    frames = x_ref[...]
    own = frames[frames.shape[0] - rows :]
    queries = jnp.dot(own, wq_ref[...], preferred_element_type=jnp.float32).astype(jnp.bfloat16)
    keys = jnp.dot(frames, wk_ref[...], preferred_element_type=jnp.float32).astype(jnp.bfloat16)
    values = jnp.dot(frames, wv_ref[...], preferred_element_type=jnp.float32).astype(jnp.bfloat16)
    result = jnp.zeros(o_ref.shape, jnp.float32)
    for head in range(heads):
        inside = (lane >= head * HEAD_DIM) & (lane < (head + 1) * HEAD_DIM)
        query = jnp.where(inside, queries, jnp.zeros_like(queries))
        scores = lax.dot_general(
            query, keys, (((1,), (1,)), ((), ())), preferred_element_type=jnp.float32
        ) * (1.0 / jnp.sqrt(jnp.float32(HEAD_DIM)))
        raised = jnp.where(allowed, jnp.exp(scores), 0.0)
        probs = (raised / jnp.sum(raised, axis=-1, keepdims=True)).astype(jnp.bfloat16)
        mixed = jnp.dot(probs, values, preferred_element_type=jnp.float32)
        result = jnp.where(inside, mixed, result)
    o_ref[...] = result.astype(o_ref.dtype)


def attend(normed_all, weights, allowed):
    rows, keys = allowed.shape
    width = normed_all.shape[1]
    tile = 128
    steps = width // tile
    return pl.pallas_call(
        attend_kernel,
        out_shape=jax.ShapeDtypeStruct((rows, width), jnp.bfloat16),
        grid=(steps,),
        in_specs=[
            pl.BlockSpec((keys, width), lambda i: (0, 0)),
            pl.BlockSpec((width, tile), lambda i: (0, i)),
            pl.BlockSpec((width, tile), lambda i: (0, i + steps)),
            pl.BlockSpec((width, tile), lambda i: (0, i + 2 * steps)),
            pl.BlockSpec((rows, keys), lambda i: (0, 0)),
        ],
        out_specs=pl.BlockSpec((rows, tile), lambda i: (0, i)),
        cost_estimate=pl.CostEstimate(
            flops=4 * rows * keys * width * tile // HEAD_DIM
            + 2 * (rows + 2 * keys) * width * width,
            transcendentals=rows * keys * width // HEAD_DIM,
            bytes_accessed=2 * (keys * width + 3 * width * width + rows * width) + 4 * rows * keys,
        ),
    )(normed_all, weights, weights, weights, allowed.astype(jnp.float32))


def on_device(
    frames, lengths, ln_attn_gain, w_qkv, w_out, ln_conv_gain, w_pw1, dw_kernel, bn_gain, bn_bias
):
    stream = frames[0]
    frame_count, model_width = stream.shape
    head_count = model_width // HEAD_DIM
    length = lax.dynamic_index_in_dim(lengths, lax.axis_index("call"), 0, keepdims=False)
    first_row = lax.axis_index(TM) * frame_count
    query_pos = first_row + jnp.arange(frame_count, dtype=jnp.int32)
    frame_valid = query_pos < length
    qkv_cols = w_qkv.shape[1]
    out_cols = w_out.shape[1]
    weights = lax.all_gather(
        jnp.concatenate([w_qkv, w_out, w_pw1], axis=1), TM, axis=0, tiled=True
    )
    prior_blocks = LEFT // frame_count
    blocks = []
    current = stream
    for hop_index in range(prior_blocks):
        current = passed_along(current, TM, 1)
        blocks.append(current)
    context_frames = jnp.concatenate(blocks[::-1] + [stream], axis=0)
    key_count = context_frames.shape[0]
    normed_all = layer_norm(context_frames, ln_attn_gain).astype(jnp.bfloat16)
    normed = normed_all[key_count - frame_count :]
    key_pos = first_row - prior_blocks * frame_count + jnp.arange(key_count, dtype=jnp.int32)
    span_first = query_pos // SPAN * SPAN
    allowed = (key_pos[None, :] >= 0) & (key_pos[None, :] >= span_first[:, None] - LEFT)
    allowed = allowed & (key_pos[None, :] < span_first[:, None] + SPAN)
    allowed = allowed & ((key_pos[None, :] < length) | (key_pos[None, :] == query_pos[:, None]))
    context = attend(normed_all, weights, allowed)
    projected = contract_with(context, weights[:, qkv_cols : qkv_cols + out_cols])
    attended = jnp.where(frame_valid[:, None], stream.astype(jnp.float32) + projected, 0.0).astype(
        jnp.bfloat16
    )
    conv_in = layer_norm(attended, ln_conv_gain).astype(jnp.bfloat16)
    expanded = contract_with(conv_in, weights[:, qkv_cols + out_cols :])
    gated = expanded[:, :model_width] * jax.nn.sigmoid(expanded[:, model_width:])
    gated = jnp.where(frame_valid[:, None], gated, 0.0).astype(jnp.bfloat16)
    padded = with_halo(gated, TM, KERNEL // 2)
    depthwise = jnp.zeros((frame_count, model_width), jnp.float32)
    for tap_index in range(KERNEL):
        depthwise = (
            depthwise
            + padded[tap_index : tap_index + frame_count].astype(jnp.float32) * dw_kernel[tap_index]
        )
    masked = jnp.where(frame_valid[:, None], depthwise, 0.0)
    moments = (jnp.sum(masked, axis=0), jnp.sum(masked * depthwise, axis=0))
    for axis in ("core", "y", "x", "call"):
        moments = lax.psum(moments, axis)
    first_moment, second_moment = moments
    count_all = jnp.sum(lengths).astype(jnp.float32)
    average = first_moment / count_all
    second = second_moment / count_all
    normal_act = (depthwise - average) * lax.rsqrt(
        second - average * average + 1e-05
    ) * bn_gain + bn_bias
    activated = normal_act * jax.nn.sigmoid(normal_act)
    conv_act = jnp.where(frame_valid[:, None], activated, 0.0).astype(jnp.bfloat16)
    return (attended[None], conv_act[None])


def physical_mesh(mesh):
    devices = mesh.devices
    calls, tms = devices.shape
    first = devices[0]
    xs = len({d.coords[0] for d in first})
    ys = len({d.coords[1] for d in first})
    cores = tms // (xs * ys)
    grid = np.array(
        [[(d.coords[0], d.coords[1], d.core_on_chip) for d in row] for row in devices]
    )
    expect = np.stack(
        np.meshgrid(np.arange(xs), np.arange(ys), np.arange(cores), indexing="ij"), -1
    ).reshape(-1, 3)
    grid = grid - grid[:, :1]
    assert (grid == expect[None]).all()
    return Mesh(devices.reshape(calls, xs, ys, cores), ("call",) + TM)


def solution(mesh):
    mesh4 = physical_mesh(mesh)
    rows = P(TM, None)
    stream = P("call", TM, None)
    return jax.shard_map(
        on_device,
        mesh=mesh4,
        in_specs=(stream, P(), P(), rows, rows, P(), rows, P(), P(), P()),
        out_specs=(stream, stream),
        check_vma=False,
    )
```

```python
import jax
import jax.numpy as jnp
import numpy as np
from jax import lax
from jax.experimental import pallas as pl
from jax.sharding import Mesh
from jax.sharding import PartitionSpec as P

HEAD_DIM = 64
SPAN = 128
LEFT = 1024
KERNEL = 9
TM = ("x", "y", "core")


def passed_along(value, axis, steps):
    count = lax.axis_size(axis)
    first, last = (max(0, -steps), min(count, count - steps))
    return lax.ppermute(value, axis, [(source, source + steps) for source in range(first, last)])


def with_halo(cells, axis, width):
    count = lax.axis_size(axis)
    ends = count - 1
    head = lax.slice_in_dim(cells, 0, width, axis=0)
    tail = lax.slice_in_dim(cells, cells.shape[0] - width, cells.shape[0], axis=0)
    return jnp.concatenate(
        [
            lax.ppermute(tail, axis, [(i, (i + 1) % count) for i in range(ends)]),
            cells,
            lax.ppermute(head, axis, [((i + 1) % count, i) for i in range(ends)]),
        ],
        axis=0,
    )


def layer_norm(values, gain_vec):
    wide = values.astype(jnp.float32)
    center = wide - jnp.mean(wide, axis=-1, keepdims=True)
    spread = jnp.mean(center * center, axis=-1, keepdims=True)
    return center * lax.rsqrt(spread + 1e-05) * gain_vec


def contract_with(left, rows_piece):
    return jnp.dot(left, rows_piece, preferred_element_type=jnp.float32)


def attend_kernel(x_ref, wq_ref, k_ref, v_ref, m_ref, o_ref):
    width = o_ref.shape[1]
    heads = width // HEAD_DIM
    allowed = m_ref[...] > 0.5
    lane = lax.broadcasted_iota(jnp.int32, (1, width), 1)
    queries = jnp.dot(x_ref[...], wq_ref[...], preferred_element_type=jnp.float32)
    queries = queries.astype(jnp.bfloat16)
    result = jnp.zeros(o_ref.shape, jnp.float32)
    for head in range(heads):
        inside = (lane >= head * HEAD_DIM) & (lane < (head + 1) * HEAD_DIM)
        query = jnp.where(inside, queries, jnp.zeros_like(queries))
        scores = lax.dot_general(
            query, k_ref[...], (((1,), (1,)), ((), ())), preferred_element_type=jnp.float32
        ) * (1.0 / jnp.sqrt(jnp.float32(HEAD_DIM)))
        raised = jnp.where(allowed, jnp.exp(scores), 0.0)
        probs = (raised / jnp.sum(raised, axis=-1, keepdims=True)).astype(jnp.bfloat16)
        mixed = jnp.dot(probs, v_ref[...], preferred_element_type=jnp.float32)
        result = jnp.where(inside, mixed, result)
    o_ref[...] = result.astype(o_ref.dtype)


def attend(normed, weights, key_value, allowed):
    rows, width = normed.shape
    keys = key_value.shape[0]
    tile = 4 * HEAD_DIM
    steps = width // tile
    return pl.pallas_call(
        attend_kernel,
        out_shape=jax.ShapeDtypeStruct((rows, width), jnp.bfloat16),
        grid=(steps,),
        in_specs=[
            pl.BlockSpec((rows, width), lambda i: (0, 0)),
            pl.BlockSpec((width, tile), lambda i: (0, i)),
            pl.BlockSpec((keys, tile), lambda i: (0, i)),
            pl.BlockSpec((keys, tile), lambda i: (0, i + steps)),
            pl.BlockSpec((rows, keys), lambda i: (0, 0)),
        ],
        out_specs=pl.BlockSpec((rows, tile), lambda i: (0, i)),
        cost_estimate=pl.CostEstimate(
            flops=4 * rows * keys * width * tile // HEAD_DIM + 2 * rows * width * width,
            transcendentals=rows * keys * width // HEAD_DIM,
            bytes_accessed=2 * (2 * rows * width + 2 * keys * width + width * width)
            + 4 * rows * keys,
        ),
    )(normed, weights, key_value, key_value, allowed.astype(jnp.float32))


def on_device(
    frames, lengths, ln_attn_gain, w_qkv, w_out, ln_conv_gain, w_pw1, dw_kernel, bn_gain, bn_bias
):
    stream = frames[0]
    frame_count, model_width = stream.shape
    head_count = model_width // HEAD_DIM
    length = lax.dynamic_index_in_dim(lengths, lax.axis_index("call"), 0, keepdims=False)
    first_row = lax.axis_index(TM) * frame_count
    query_pos = first_row + jnp.arange(frame_count, dtype=jnp.int32)
    frame_valid = query_pos < length
    qkv_cols = w_qkv.shape[1]
    out_cols = w_out.shape[1]
    weights = lax.all_gather(
        jnp.concatenate([w_qkv, w_out, w_pw1], axis=1), TM, axis=0, tiled=True
    )
    prior_blocks = LEFT // frame_count
    blocks = []
    current = stream
    for hop_index in range(prior_blocks):
        current = passed_along(current, TM, 1)
        blocks.append(current)
    context_frames = jnp.concatenate(blocks[::-1] + [stream], axis=0)
    key_count = context_frames.shape[0]
    normed_all = layer_norm(context_frames, ln_attn_gain).astype(jnp.bfloat16)
    normed = normed_all[key_count - frame_count :]
    key_value = contract_with(normed_all, weights[:, model_width:qkv_cols]).astype(jnp.bfloat16)
    key_pos = first_row - prior_blocks * frame_count + jnp.arange(key_count, dtype=jnp.int32)
    span_first = query_pos // SPAN * SPAN
    allowed = (key_pos[None, :] >= 0) & (key_pos[None, :] >= span_first[:, None] - LEFT)
    allowed = allowed & (key_pos[None, :] < span_first[:, None] + SPAN)
    allowed = allowed & ((key_pos[None, :] < length) | (key_pos[None, :] == query_pos[:, None]))
    context = attend(normed, weights, key_value, allowed)
    projected = contract_with(context, weights[:, qkv_cols : qkv_cols + out_cols])
    attended = jnp.where(frame_valid[:, None], stream.astype(jnp.float32) + projected, 0.0).astype(
        jnp.bfloat16
    )
    conv_in = layer_norm(attended, ln_conv_gain).astype(jnp.bfloat16)
    expanded = contract_with(conv_in, weights[:, qkv_cols + out_cols :])
    gated = expanded[:, :model_width] * jax.nn.sigmoid(expanded[:, model_width:])
    gated = jnp.where(frame_valid[:, None], gated, 0.0).astype(jnp.bfloat16)
    padded = with_halo(gated, TM, KERNEL // 2)
    depthwise = jnp.zeros((frame_count, model_width), jnp.float32)
    for tap_index in range(KERNEL):
        depthwise = (
            depthwise
            + padded[tap_index : tap_index + frame_count].astype(jnp.float32) * dw_kernel[tap_index]
        )
    masked = jnp.where(frame_valid[:, None], depthwise, 0.0)
    moments = (jnp.sum(masked, axis=0), jnp.sum(masked * depthwise, axis=0))
    for axis in ("core", "y", "x", "call"):
        moments = lax.psum(moments, axis)
    first_moment, second_moment = moments
    count_all = jnp.sum(lengths).astype(jnp.float32)
    average = first_moment / count_all
    second = second_moment / count_all
    normal_act = (depthwise - average) * lax.rsqrt(
        second - average * average + 1e-05
    ) * bn_gain + bn_bias
    activated = normal_act * jax.nn.sigmoid(normal_act)
    conv_act = jnp.where(frame_valid[:, None], activated, 0.0).astype(jnp.bfloat16)
    return (attended[None], conv_act[None])


def physical_mesh(mesh):
    devices = mesh.devices
    calls, tms = devices.shape
    first = devices[0]
    xs = len({d.coords[0] for d in first})
    ys = len({d.coords[1] for d in first})
    cores = tms // (xs * ys)
    grid = np.array(
        [[(d.coords[0], d.coords[1], d.core_on_chip) for d in row] for row in devices]
    )
    expect = np.stack(
        np.meshgrid(np.arange(xs), np.arange(ys), np.arange(cores), indexing="ij"), -1
    ).reshape(-1, 3)
    grid = grid - grid[:, :1]
    assert (grid == expect[None]).all()
    return Mesh(devices.reshape(calls, xs, ys, cores), ("call",) + TM)


def solution(mesh):
    mesh4 = physical_mesh(mesh)
    rows = P(TM, None)
    stream = P("call", TM, None)
    return jax.shard_map(
        on_device,
        mesh=mesh4,
        in_specs=(stream, P(), P(), rows, rows, P(), rows, P(), P(), P()),
        out_specs=(stream, stream),
        check_vma=False,
    )
```

```python
import jax
import jax.numpy as jnp
import numpy as np
from jax import lax
from jax.experimental import pallas as pl
from jax.sharding import Mesh
from jax.sharding import PartitionSpec as P

HEAD_DIM = 64
SPAN = 128
LEFT = 1024
KERNEL = 9
TM = ("x", "y", "core")


def passed_along(value, axis, steps):
    count = lax.axis_size(axis)
    first, last = (max(0, -steps), min(count, count - steps))
    return lax.ppermute(value, axis, [(source, source + steps) for source in range(first, last)])


def with_halo(cells, axis, width):
    count = lax.axis_size(axis)
    ends = count - 1
    head = lax.slice_in_dim(cells, 0, width, axis=0)
    tail = lax.slice_in_dim(cells, cells.shape[0] - width, cells.shape[0], axis=0)
    return jnp.concatenate(
        [
            lax.ppermute(tail, axis, [(i, (i + 1) % count) for i in range(ends)]),
            cells,
            lax.ppermute(head, axis, [((i + 1) % count, i) for i in range(ends)]),
        ],
        axis=0,
    )


def layer_norm(values, gain_vec):
    wide = values.astype(jnp.float32)
    center = wide - jnp.mean(wide, axis=-1, keepdims=True)
    spread = jnp.mean(center * center, axis=-1, keepdims=True)
    return center * lax.rsqrt(spread + 1e-05) * gain_vec


def contract_with(left, rows_piece):
    return jnp.dot(left, rows_piece, preferred_element_type=jnp.float32)


def attend_kernel(x_ref, wq_ref, k_ref, v_ref, m_ref, o_ref):
    width = o_ref.shape[1]
    heads = width // HEAD_DIM
    allowed = m_ref[...] > 0.5
    lane = lax.broadcasted_iota(jnp.int32, (1, width), 1)
    queries = jnp.dot(x_ref[...], wq_ref[...], preferred_element_type=jnp.float32)
    queries = queries.astype(jnp.bfloat16)
    result = jnp.zeros(o_ref.shape, jnp.float32)
    for head in range(heads):
        inside = (lane >= head * HEAD_DIM) & (lane < (head + 1) * HEAD_DIM)
        query = jnp.where(inside, queries, jnp.zeros_like(queries))
        scores = lax.dot_general(
            query, k_ref[...], (((1,), (1,)), ((), ())), preferred_element_type=jnp.float32
        ) * (1.0 / jnp.sqrt(jnp.float32(HEAD_DIM)))
        raised = jnp.where(allowed, jnp.exp(scores), 0.0)
        probs = (raised / jnp.sum(raised, axis=-1, keepdims=True)).astype(jnp.bfloat16)
        mixed = jnp.dot(probs, v_ref[...], preferred_element_type=jnp.float32)
        result = jnp.where(inside, mixed, result)
    o_ref[...] = result.astype(o_ref.dtype)


def attend(normed, weights, key_value, allowed):
    rows, width = normed.shape
    keys = key_value.shape[0]
    tile = 128
    steps = width // tile
    return pl.pallas_call(
        attend_kernel,
        out_shape=jax.ShapeDtypeStruct((rows, width), jnp.bfloat16),
        grid=(steps,),
        in_specs=[
            pl.BlockSpec((rows, width), lambda i: (0, 0)),
            pl.BlockSpec((width, tile), lambda i: (0, i)),
            pl.BlockSpec((keys, tile), lambda i: (0, i)),
            pl.BlockSpec((keys, tile), lambda i: (0, i + steps)),
            pl.BlockSpec((rows, keys), lambda i: (0, 0)),
        ],
        out_specs=pl.BlockSpec((rows, tile), lambda i: (0, i)),
        cost_estimate=pl.CostEstimate(
            flops=4 * rows * keys * width * tile // HEAD_DIM + 2 * rows * width * width,
            transcendentals=rows * keys * width // HEAD_DIM,
            bytes_accessed=2 * (2 * rows * width + 2 * keys * width + width * width)
            + 4 * rows * keys,
        ),
    )(normed, weights, key_value, key_value, allowed.astype(jnp.float32))


def on_device(
    frames, lengths, ln_attn_gain, w_qkv, w_out, ln_conv_gain, w_pw1, dw_kernel, bn_gain, bn_bias
):
    stream = frames[0]
    frame_count, model_width = stream.shape
    head_count = model_width // HEAD_DIM
    length = lax.dynamic_index_in_dim(lengths, lax.axis_index("call"), 0, keepdims=False)
    first_row = lax.axis_index(TM) * frame_count
    core = lax.axis_index("core")
    query_pos = first_row + jnp.arange(frame_count, dtype=jnp.int32)
    frame_valid = query_pos < length
    qkv_cols = w_qkv.shape[1]
    out_cols = w_out.shape[1]
    weights = lax.all_gather(
        jnp.concatenate([w_qkv, w_out, w_pw1], axis=1), TM, axis=0, tiled=True
    )
    prior_blocks = LEFT // frame_count
    blocks = []
    current = stream
    for hop_index in range(prior_blocks):
        current = passed_along(current, TM, 1)
        blocks.append(current)
    context_frames = jnp.concatenate(blocks[::-1] + [stream], axis=0)
    key_count = context_frames.shape[0]
    normed_all = layer_norm(context_frames, ln_attn_gain).astype(jnp.bfloat16)
    normed = normed_all[key_count - frame_count :]
    key_value = contract_with(normed_all, weights[:, model_width:qkv_cols]).astype(jnp.bfloat16)
    key_pos = first_row - prior_blocks * frame_count + jnp.arange(key_count, dtype=jnp.int32)
    span_first = query_pos // SPAN * SPAN
    allowed = (key_pos[None, :] >= 0) & (key_pos[None, :] >= span_first[:, None] - LEFT)
    allowed = allowed & (key_pos[None, :] < span_first[:, None] + SPAN)
    allowed = allowed & ((key_pos[None, :] < length) | (key_pos[None, :] == query_pos[:, None]))
    context = attend(normed, weights, key_value, allowed)
    projected = contract_with(context, weights[:, qkv_cols : qkv_cols + out_cols])
    attended = jnp.where(frame_valid[:, None], stream.astype(jnp.float32) + projected, 0.0).astype(
        jnp.bfloat16
    )
    conv_in = layer_norm(attended, ln_conv_gain).astype(jnp.bfloat16)
    expanded = contract_with(conv_in, weights[:, qkv_cols + out_cols :])
    gated = expanded[:, :model_width] * jax.nn.sigmoid(expanded[:, model_width:])
    gated = jnp.where(frame_valid[:, None], gated, 0.0).astype(jnp.bfloat16)
    width = KERNEL // 2
    head, tail = gated[:width], gated[frame_count - width :]
    count = lax.axis_size(TM)
    from_partner = lax.ppermute(jnp.where(core == 0, tail, head), "core", [(0, 1), (1, 0)])
    chip_pairs = [(i, i + 1) if i % 2 else (i, i - 1) for i in range(count)]
    chip_pairs = [(a, b) for a, b in chip_pairs if 0 <= b < count]
    from_chip = lax.ppermute(jnp.where(core == 1, tail, head), TM, chip_pairs)
    before = jnp.where(core == 1, from_partner, from_chip)
    after = jnp.where(core == 0, from_partner, from_chip)
    padded = jnp.concatenate([before, gated, after], axis=0)
    depthwise = jnp.zeros((frame_count, model_width), jnp.float32)
    for tap_index in range(KERNEL):
        depthwise = (
            depthwise
            + padded[tap_index : tap_index + frame_count].astype(jnp.float32) * dw_kernel[tap_index]
        )
    masked = jnp.where(frame_valid[:, None], depthwise, 0.0)
    moments = (jnp.sum(masked, axis=0), jnp.sum(masked * depthwise, axis=0))
    for axis in ("core", "y", "x", "call"):
        moments = lax.psum(moments, axis)
    first_moment, second_moment = moments
    count_all = jnp.sum(lengths).astype(jnp.float32)
    average = first_moment / count_all
    second = second_moment / count_all
    normal_act = (depthwise - average) * lax.rsqrt(
        second - average * average + 1e-05
    ) * bn_gain + bn_bias
    activated = normal_act * jax.nn.sigmoid(normal_act)
    conv_act = jnp.where(frame_valid[:, None], activated, 0.0).astype(jnp.bfloat16)
    return (attended[None], conv_act[None])


def physical_mesh(mesh):
    devices = mesh.devices
    calls, tms = devices.shape
    first = devices[0]
    xs = len({d.coords[0] for d in first})
    ys = len({d.coords[1] for d in first})
    cores = tms // (xs * ys)
    grid = np.array(
        [[(d.coords[0], d.coords[1], d.core_on_chip) for d in row] for row in devices]
    )
    expect = np.stack(
        np.meshgrid(np.arange(xs), np.arange(ys), np.arange(cores), indexing="ij"), -1
    ).reshape(-1, 3)
    grid = grid - grid[:, :1]
    assert (grid == expect[None]).all()
    return Mesh(devices.reshape(calls, xs, ys, cores), ("call",) + TM)


def solution(mesh):
    mesh4 = physical_mesh(mesh)
    rows = P(TM, None)
    stream = P("call", TM, None)
    return jax.shard_map(
        on_device,
        mesh=mesh4,
        in_specs=(stream, P(), P(), rows, rows, P(), rows, P(), P(), P()),
        out_specs=(stream, stream),
        check_vma=False,
    )
```

```python
import jax
import jax.numpy as jnp
import numpy as np
from jax import lax
from jax.experimental import pallas as pl
from jax.sharding import Mesh
from jax.sharding import PartitionSpec as P

HEAD_DIM = 64
SPAN = 128
LEFT = 1024
KERNEL = 9
TM = ("x", "ya", "yb", "core")
CALL = ("za", "zb")


def passed_along(value, axis, steps):
    count = lax.axis_size(axis)
    first, last = (max(0, -steps), min(count, count - steps))
    return lax.ppermute(value, axis, [(source, source + steps) for source in range(first, last)])


def with_halo(cells, axis, width):
    count = lax.axis_size(axis)
    ends = count - 1
    head = lax.slice_in_dim(cells, 0, width, axis=0)
    tail = lax.slice_in_dim(cells, cells.shape[0] - width, cells.shape[0], axis=0)
    return jnp.concatenate(
        [
            lax.ppermute(tail, axis, [(i, (i + 1) % count) for i in range(ends)]),
            cells,
            lax.ppermute(head, axis, [((i + 1) % count, i) for i in range(ends)]),
        ],
        axis=0,
    )


def layer_norm(values, gain_vec):
    wide = values.astype(jnp.float32)
    center = wide - jnp.mean(wide, axis=-1, keepdims=True)
    spread = jnp.mean(center * center, axis=-1, keepdims=True)
    return center * lax.rsqrt(spread + 1e-05) * gain_vec


def contract_with(left, rows_piece):
    return jnp.dot(left, rows_piece, preferred_element_type=jnp.float32)


def attend_kernel(x_ref, wq_ref, k_ref, v_ref, m_ref, o_ref):
    width = o_ref.shape[1]
    heads = width // HEAD_DIM
    allowed = m_ref[...] > 0.5
    lane = lax.broadcasted_iota(jnp.int32, (1, width), 1)
    queries = jnp.dot(x_ref[...], wq_ref[...], preferred_element_type=jnp.float32)
    queries = queries.astype(jnp.bfloat16)
    result = jnp.zeros(o_ref.shape, jnp.float32)
    for head in range(heads):
        inside = (lane >= head * HEAD_DIM) & (lane < (head + 1) * HEAD_DIM)
        query = jnp.where(inside, queries, jnp.zeros_like(queries))
        scores = lax.dot_general(
            query, k_ref[...], (((1,), (1,)), ((), ())), preferred_element_type=jnp.float32
        ) * (1.0 / jnp.sqrt(jnp.float32(HEAD_DIM)))
        raised = jnp.where(allowed, jnp.exp(scores), 0.0)
        probs = (raised / jnp.sum(raised, axis=-1, keepdims=True)).astype(jnp.bfloat16)
        mixed = jnp.dot(probs, v_ref[...], preferred_element_type=jnp.float32)
        result = jnp.where(inside, mixed, result)
    o_ref[...] = result.astype(o_ref.dtype)


def attend(normed, weights, key_value, allowed):
    rows, width = normed.shape
    keys = key_value.shape[0]
    tile = 128
    steps = width // tile
    return pl.pallas_call(
        attend_kernel,
        out_shape=jax.ShapeDtypeStruct((rows, width), jnp.bfloat16),
        grid=(steps,),
        in_specs=[
            pl.BlockSpec((rows, width), lambda i: (0, 0)),
            pl.BlockSpec((width, tile), lambda i: (0, i)),
            pl.BlockSpec((keys, tile), lambda i: (0, i)),
            pl.BlockSpec((keys, tile), lambda i: (0, i + steps)),
            pl.BlockSpec((rows, keys), lambda i: (0, 0)),
        ],
        out_specs=pl.BlockSpec((rows, tile), lambda i: (0, i)),
        cost_estimate=pl.CostEstimate(
            flops=4 * rows * keys * width * tile // HEAD_DIM + 2 * rows * width * width,
            transcendentals=rows * keys * width // HEAD_DIM,
            bytes_accessed=2 * (2 * rows * width + 2 * keys * width + width * width)
            + 4 * rows * keys,
        ),
    )(normed, weights, key_value, key_value, allowed.astype(jnp.float32))


def on_device(
    frames, lengths, ln_attn_gain, w_qkv, w_out, ln_conv_gain, w_pw1, dw_kernel, bn_gain, bn_bias
):
    stream = frames[0]
    frame_count, model_width = stream.shape
    head_count = model_width // HEAD_DIM
    length = lax.dynamic_index_in_dim(lengths, lax.axis_index(CALL), 0, keepdims=False)
    first_row = lax.axis_index(TM) * frame_count
    query_pos = first_row + jnp.arange(frame_count, dtype=jnp.int32)
    frame_valid = query_pos < length
    qkv_cols = w_qkv.shape[1]
    out_cols = w_out.shape[1]
    weights = lax.all_gather(
        jnp.concatenate([w_qkv, w_out, w_pw1], axis=1), TM, axis=0, tiled=True
    )
    prior_blocks = LEFT // frame_count
    blocks = []
    current = stream
    for hop_index in range(prior_blocks):
        current = passed_along(current, TM, 1)
        blocks.append(current)
    context_frames = jnp.concatenate(blocks[::-1] + [stream], axis=0)
    key_count = context_frames.shape[0]
    normed_all = layer_norm(context_frames, ln_attn_gain).astype(jnp.bfloat16)
    normed = normed_all[key_count - frame_count :]
    key_value = contract_with(normed_all, weights[:, model_width:qkv_cols]).astype(jnp.bfloat16)
    key_pos = first_row - prior_blocks * frame_count + jnp.arange(key_count, dtype=jnp.int32)
    span_first = query_pos // SPAN * SPAN
    allowed = (key_pos[None, :] >= 0) & (key_pos[None, :] >= span_first[:, None] - LEFT)
    allowed = allowed & (key_pos[None, :] < span_first[:, None] + SPAN)
    allowed = allowed & ((key_pos[None, :] < length) | (key_pos[None, :] == query_pos[:, None]))
    context = attend(normed, weights, key_value, allowed)
    projected = contract_with(context, weights[:, qkv_cols : qkv_cols + out_cols])
    attended = jnp.where(frame_valid[:, None], stream.astype(jnp.float32) + projected, 0.0).astype(
        jnp.bfloat16
    )
    conv_in = layer_norm(attended, ln_conv_gain).astype(jnp.bfloat16)
    expanded = contract_with(conv_in, weights[:, qkv_cols + out_cols :])
    gated = expanded[:, :model_width] * jax.nn.sigmoid(expanded[:, model_width:])
    gated = jnp.where(frame_valid[:, None], gated, 0.0).astype(jnp.bfloat16)
    padded = with_halo(gated, TM, KERNEL // 2)
    depthwise = jnp.zeros((frame_count, model_width), jnp.float32)
    for tap_index in range(KERNEL):
        depthwise = (
            depthwise
            + padded[tap_index : tap_index + frame_count].astype(jnp.float32) * dw_kernel[tap_index]
        )
    masked = jnp.where(frame_valid[:, None], depthwise, 0.0)
    moments = (jnp.sum(masked, axis=0), jnp.sum(masked * depthwise, axis=0))
    for axis in ("core", "yb", "ya", "x", "zb", "za"):
        moments = lax.psum(moments, axis)
    first_moment, second_moment = moments
    count_all = jnp.sum(lengths).astype(jnp.float32)
    average = first_moment / count_all
    second = second_moment / count_all
    normal_act = (depthwise - average) * lax.rsqrt(
        second - average * average + 1e-05
    ) * bn_gain + bn_bias
    activated = normal_act * jax.nn.sigmoid(normal_act)
    conv_act = jnp.where(frame_valid[:, None], activated, 0.0).astype(jnp.bfloat16)
    return (attended[None], conv_act[None])


def physical_mesh(mesh):
    devices = mesh.devices
    calls, tms = devices.shape
    first = devices[0]
    xs = len({d.coords[0] for d in first})
    ys = len({d.coords[1] for d in first})
    cores = tms // (xs * ys)
    grid = np.array(
        [[(d.coords[0], d.coords[1], d.core_on_chip) for d in row] for row in devices]
    )
    expect = np.stack(
        np.meshgrid(np.arange(xs), np.arange(ys), np.arange(cores), indexing="ij"), -1
    ).reshape(-1, 3)
    grid = grid - grid[:, :1]
    assert (grid == expect[None]).all()
    return Mesh(devices.reshape(calls // 2, 2, xs, ys // 2, 2, cores), CALL + TM)


def solution(mesh):
    mesh4 = physical_mesh(mesh)
    rows = P(TM, None)
    stream = P(CALL, TM, None)
    return jax.shard_map(
        on_device,
        mesh=mesh4,
        in_specs=(stream, P(), P(), rows, rows, P(), rows, P(), P(), P()),
        out_specs=(stream, stream),
        check_vma=False,
    )
```
